1024 devices in a mesh: seq: 64 (over z, x), fsdp: 16 (over y, core).
Axes of the slice: x: 8, y: 8, z: 8, core: 2. Of those that a mesh axis runs over, the one named last changes fastest.
Arguments:
- query_act: bfloat16 [16384, 8192], P('seq', 'fsdp'), may hold values from -6 to 6
- key_act: bfloat16 [16384, 8192], P('seq', 'fsdp'), may hold values from -6 to 6
- value_act: bfloat16 [16384, 8192], P('seq', 'fsdp'), may hold values from -6 to 6
- gate_act: bfloat16 [16384, 8192], P('seq', 'fsdp'), may hold values from -6 to 6
- rate_index: int32 [64], P('fsdp'), may hold values from 0 to 63, each once
- norm_gain: float32 [8192], P('fsdp'), may hold values from 0.1 to 1.9
- out_weight: bfloat16 [8192, 6144], P('fsdp'), may hold values from -0.0625 to 0.0625
Outputs:
- layer_out: bfloat16 [16384, 6144], P(('seq', 'fsdp'))
The draws below stay inside these ranges and needn't reach their ends.
Inputs may be any that keep to these rules, and one draw needn't show every extreme that they name: `rate_index`: each head index of 0 to 63 appears once.
All inputs are finite; a program needn't handle non-finite values.
Results may differ from the reference program's by a relative error of at most 0.018.
Values may be sent and summed in bfloat16 or wider, within the bound.
No kernel may reach another device: no remote copies, remote signals or barrier semaphores. Data moves between devices by JAX's collectives and lax.ppermute only.
A program may use at most 64 MiB of HBM per device.

```python
import math
import jax
import jax.numpy as jnp
from jax import lax

D = 6144
HEADS = 64
HEAD_DIM = 128
TOK_DEV = 256
HEADS_DEV = 4
SEQLEN = 16384
N_SEQ = 64
N_FSDP = 16


def block_scale(rng, dims, cuts, least, high):
    loudness = 1.0
    for dim, blocks in cuts:
        draws = jax.random.uniform(jax.random.fold_in(jax.random.fold_in(rng, 6), dim), (blocks,), jnp.float32, least / len(cuts), high / len(cuts))
        loudness = loudness * jnp.repeat(jnp.exp(draws), dims[dim] // blocks).reshape((-1,) + (1,) * (len(dims) - 1 - dim))
    return loudness


def centred(stream_key, shape, scale, limit, cuts=(), dtype=jnp.bfloat16):
    array = jax.random.normal(stream_key, shape, jnp.float32) * scale
    if len(cuts) > 0:
        array = block_scale(stream_key, shape, cuts, -0.22, 0.18) * array
    return jnp.clip(array, min=-limit, max=limit).astype(dtype)


def setup_inputs(seed: int = 0) -> dict:
    key_of = jax.random.split(jax.random.key(seed), 8)
    query_act = centred(key_of[0], (SEQLEN, HEADS * HEAD_DIM), 1.0, 6.0, ((0, 64), (1, 16)))
    key_act = centred(key_of[1], (SEQLEN, HEADS * HEAD_DIM), 1.0, 6.0, ((0, 64), (1, 16)))
    value_act = centred(key_of[2], (SEQLEN, HEADS * HEAD_DIM), 1.0, 6.0, ((0, 64), (1, 16)))
    gate_act = centred(key_of[3], (SEQLEN, HEADS * HEAD_DIM), 1.5, 6.0, ((0, 64), (1, 16)))
    rate_index = jax.random.permutation(key_of[4], HEADS).astype(jnp.int32)
    norm_gain = jnp.clip(1.0 + 0.18 * jax.random.normal(key_of[5], (HEADS * HEAD_DIM,), jnp.float32), 0.1, 1.9)
    out_weight = centred(key_of[6], (HEADS * HEAD_DIM, D), (HEADS * HEAD_DIM) ** -0.5, 0.0625, ((0, 16),))
    return dict(query_act=query_act, key_act=key_act, value_act=value_act, gate_act=gate_act, rate_index=rate_index, norm_gain=norm_gain, out_weight=out_weight)


layer_factor = 1.0 - 78.0 / 79.0 + 1e-05

def decay_slopes(rate_index):
    exponent = -8.0 * (rate_index.astype(jnp.float32) + 1.0) / HEADS
    return jnp.exp(exponent * math.log(2.0)) * layer_factor

def span_terms(query_rows, key_rows, value_rows, slopes):
    tok_count = query_rows.shape[0]
    position = jnp.arange(tok_count).astype(jnp.float32)
    offset = position[:, None] - position[None, :]
    causal = jnp.where(offset[None] >= 0.0, jnp.exp(-slopes[:, None, None] * jnp.maximum(offset, 0.0)[None]), 0.0)
    scores = jnp.einsum('thd,shd->hts', query_rows.astype(jnp.float32), key_rows.astype(jnp.float32))
    weighted = (scores * causal).astype(jnp.bfloat16)
    intra_part = jnp.einsum('hts,she->the', weighted.astype(jnp.float32), value_rows.astype(jnp.float32))
    to_end = jnp.exp(-slopes[None, :] * (tok_count - 1.0 - position)[:, None])
    key_scaled = (key_rows.astype(jnp.float32) * to_end[:, :, None]).astype(jnp.bfloat16)
    local_state = jnp.einsum('thd,the->hde', key_scaled.astype(jnp.float32), value_rows.astype(jnp.float32))
    from_start = jnp.exp(-slopes[None, :] * (position + 1.0)[:, None])
    return (intra_part, local_state, from_start)

def normalize_gate(intra_part, from_start, query_rows, incoming, gate_rows, gain_table):
    inter_part = jnp.einsum('thd,hde->the', query_rows.astype(jnp.float32), incoming, precision=lax.Precision.HIGHEST)
    attended = intra_part + from_start[:, :, None] * inter_part
    square_sum = lax.optimization_barrier(jnp.sum(attended * attended, axis=(1, 2), keepdims=True))
    inv_rms = lax.rsqrt(square_sum / (HEADS * HEAD_DIM) + 1e-06)
    normed = attended * inv_rms * gain_table[None] * jax.nn.sigmoid(gate_rows.astype(jnp.float32))
    return normed.reshape(query_rows.shape[0], -1).astype(jnp.bfloat16)

def reference(query_act, key_act, value_act, gate_act, rate_index, norm_gain, out_weight):
    seq_total = query_act.shape[0]
    slopes = decay_slopes(rate_index)
    carry_decay = jnp.exp(-slopes * TOK_DEV)
    block_shape = (N_SEQ, TOK_DEV, HEADS, HEAD_DIM)
    query_blocks = query_act.reshape(block_shape)
    key_blocks = key_act.reshape(block_shape)
    value_blocks = value_act.reshape(block_shape)
    gate_blocks = gate_act.reshape(block_shape)
    gain_table = norm_gain.reshape(HEADS, HEAD_DIM)
    weight_groups = out_weight.reshape(N_FSDP, HEADS_DEV * HEAD_DIM, D)

    def span_step(incoming, blocks):
        query_rows, key_rows, value_rows, gate_rows = blocks
        intra_part, local_state, from_start = span_terms(query_rows, key_rows, value_rows, slopes)
        hidden = normalize_gate(intra_part, from_start, query_rows, incoming, gate_rows, gain_table)
        hidden_groups = hidden.reshape(TOK_DEV, N_FSDP, HEADS_DEV * HEAD_DIM)

        def add_group(group_index, summed):
            rounded = jnp.dot(hidden_groups[:, group_index], weight_groups[group_index], preferred_element_type=jnp.float32).astype(jnp.bfloat16)
            rounded = lax.optimization_barrier(rounded)
            return summed + rounded.astype(jnp.float32)
        summed = lax.fori_loop(0, N_FSDP, add_group, jnp.zeros((TOK_DEV, D), jnp.float32))
        new_state = carry_decay[:, None, None] * incoming + local_state
        return (new_state, summed.astype(jnp.bfloat16))
    zero_state = jnp.zeros((HEADS, HEAD_DIM, HEAD_DIM), jnp.float32)
    final_state, out_blocks = lax.scan(span_step, zero_state, (query_blocks, key_blocks, value_blocks, gate_blocks))
    return out_blocks.reshape(seq_total, D)
```

```python
import math

import jax
import jax.numpy as jnp
from jax import lax
from jax.sharding import PartitionSpec as P

HEADS = 64
HEAD_DIM = 128


layer_factor = 1.0 - 78.0 / 79.0 + 1e-05


def decay_slopes(rate_index):
    exponent = -8.0 * (rate_index.astype(jnp.float32) + 1.0) / HEADS
    return jnp.exp(exponent * math.log(2.0)) * layer_factor


def span_terms(query_rows, key_rows, value_rows, slopes):
    tok_count = query_rows.shape[0]
    position = jnp.arange(tok_count).astype(jnp.float32)
    offset = position[:, None] - position[None, :]
    causal = jnp.where(
        offset[None] >= 0.0, jnp.exp(-slopes[:, None, None] * jnp.maximum(offset, 0.0)[None]), 0.0
    )
    scores = jnp.einsum("thd,shd->hts", query_rows, key_rows, preferred_element_type=jnp.float32)
    weighted = (scores * causal).astype(jnp.bfloat16)
    intra_part = jnp.einsum(
        "hts,she->the", weighted, value_rows, preferred_element_type=jnp.float32
    )
    to_end = jnp.exp(-slopes[None, :] * (tok_count - 1.0 - position)[:, None])
    key_scaled = (key_rows.astype(jnp.float32) * to_end[:, :, None]).astype(jnp.bfloat16)
    local_state = jnp.einsum(
        "thd,the->hde", key_scaled, value_rows, preferred_element_type=jnp.float32
    )
    from_start = jnp.exp(-slopes[None, :] * (position + 1.0)[:, None])
    return (intra_part, local_state, from_start)


def decayed_scan(local_state, slopes, tok_count, axis):
    peers = lax.axis_size(axis)
    total = local_state
    shift = 1
    while shift < peers:
        decay = jnp.exp(-slopes * (tok_count * shift))
        moved = lax.ppermute(total, axis, perm=[(i, i + shift) for i in range(peers - shift)])
        total = total + decay[:, None, None] * moved
        shift *= 2
    undo = jnp.exp(slopes * tok_count)
    return (total - local_state) * undo[:, None, None]


def per_device(query_act, key_act, value_act, gate_act, rate_index, norm_gain, out_weight):
    tok_count = query_act.shape[0]
    heads_here = rate_index.shape[0]
    slopes = decay_slopes(rate_index)
    span_shape = (tok_count, heads_here, HEAD_DIM)
    query_rows = query_act.reshape(span_shape)
    key_rows = key_act.reshape(span_shape)
    value_rows = value_act.reshape(span_shape)
    gate_rows = gate_act.reshape(span_shape)
    gain_table = norm_gain.reshape(heads_here, HEAD_DIM)
    intra_part, local_state, from_start = span_terms(query_rows, key_rows, value_rows, slopes)
    incoming = decayed_scan(local_state, slopes, tok_count, "seq")
    inter_part = jnp.einsum(
        "thd,hde->the", query_rows.astype(jnp.float32), incoming, precision=lax.Precision.HIGHEST
    )
    attended = intra_part + from_start[:, :, None] * inter_part
    local_squares = jnp.sum(attended * attended, axis=(1, 2))
    gated = attended * gain_table[None] * jax.nn.sigmoid(gate_rows.astype(jnp.float32))
    gated = gated.reshape(tok_count, -1).astype(jnp.bfloat16)
    projected = jnp.dot(gated, out_weight, preferred_element_type=jnp.float32).astype(jnp.bfloat16)
    summed = lax.psum_scatter(projected, "fsdp", scatter_dimension=0, tiled=True)
    square_sum = lax.psum_scatter(local_squares, "fsdp", scatter_dimension=0, tiled=True)
    inv_rms = lax.rsqrt(square_sum / (HEADS * HEAD_DIM) + 1e-06)
    return (summed.astype(jnp.float32) * inv_rms[:, None]).astype(jnp.bfloat16)


def solution(mesh):
    placed = (
        P("seq", "fsdp"),
        P("seq", "fsdp"),
        P("seq", "fsdp"),
        P("seq", "fsdp"),
        P("fsdp"),
        P("fsdp"),
        P("fsdp", None),
    )
    return jax.shard_map(
        per_device, mesh=mesh, in_specs=placed, out_specs=P(("seq", "fsdp"), None), check_vma=False
    )
```

```python
import math

import jax
import jax.numpy as jnp
from jax import lax
from jax.sharding import PartitionSpec as P

HEADS = 64
HEAD_DIM = 128


layer_factor = 1.0 - 78.0 / 79.0 + 1e-05


def decay_slopes(rate_index):
    exponent = -8.0 * (rate_index.astype(jnp.float32) + 1.0) / HEADS
    return jnp.exp(exponent * math.log(2.0)) * layer_factor


def span_terms(query_rows, key_rows, value_rows, slopes):
    tok_count = query_rows.shape[0]
    position = jnp.arange(tok_count).astype(jnp.float32)
    offset = position[:, None] - position[None, :]
    causal = jnp.where(
        offset[None] >= 0.0, jnp.exp(-slopes[:, None, None] * jnp.maximum(offset, 0.0)[None]), 0.0
    )
    scores = jnp.einsum("thd,shd->hts", query_rows, key_rows, preferred_element_type=jnp.float32)
    weighted = (scores * causal).astype(jnp.bfloat16)
    intra_part = jnp.einsum(
        "hts,she->the", weighted, value_rows, preferred_element_type=jnp.float32
    )
    to_end = jnp.exp(-slopes[None, :] * (tok_count - 1.0 - position)[:, None])
    key_scaled = (key_rows.astype(jnp.float32) * to_end[:, :, None]).astype(jnp.bfloat16)
    local_state = jnp.einsum(
        "thd,the->hde", key_scaled, value_rows, preferred_element_type=jnp.float32
    )
    from_start = jnp.exp(-slopes[None, :] * (position + 1.0)[:, None])
    return (intra_part, local_state, from_start)


def decayed_scan(local_state, slopes, tok_count, axis):
    peers = lax.axis_size(axis)
    total = local_state
    shift = 1
    while shift < peers:
        decay = jnp.exp(-slopes * (tok_count * shift))
        moved = lax.ppermute(total, axis, perm=[(i, i + shift) for i in range(peers - shift)])
        total = total + decay[:, None, None] * moved
        shift *= 2
    undo = jnp.exp(slopes * tok_count)
    return (total - local_state) * undo[:, None, None]


def per_device(query_act, key_act, value_act, gate_act, rate_index, norm_gain, out_weight):
    tok_count = query_act.shape[0]
    heads_here = rate_index.shape[0]
    slopes = decay_slopes(rate_index)
    span_shape = (tok_count, heads_here, HEAD_DIM)
    query_rows = query_act.reshape(span_shape)
    key_rows = key_act.reshape(span_shape)
    value_rows = value_act.reshape(span_shape)
    gate_rows = gate_act.reshape(span_shape)
    gain_table = norm_gain.reshape(heads_here, HEAD_DIM)
    intra_part, local_state, from_start = span_terms(query_rows, key_rows, value_rows, slopes)
    incoming = decayed_scan(local_state, slopes, tok_count, ("sz", "sx"))
    inter_part = jnp.einsum(
        "thd,hde->the", query_rows.astype(jnp.float32), incoming, precision=lax.Precision.HIGHEST
    )
    attended = intra_part + from_start[:, :, None] * inter_part
    local_squares = jnp.sum(attended * attended, axis=(1, 2))
    gated = attended * gain_table[None] * jax.nn.sigmoid(gate_rows.astype(jnp.float32))
    gated = gated.reshape(tok_count, -1).astype(jnp.bfloat16)
    projected = jnp.dot(gated, out_weight, preferred_element_type=jnp.float32).astype(jnp.bfloat16)
    lanes = projected.shape[1]
    cores = lax.axis_size("fc")
    chips = lax.axis_size("fy")
    projected = projected.reshape(chips, cores, tok_count // (chips * cores), lanes)
    projected = projected.transpose(1, 0, 2, 3).reshape(tok_count, lanes)
    summed = lax.psum_scatter(projected, "fc", scatter_dimension=0, tiled=True)
    summed = lax.psum_scatter(summed, "fy", scatter_dimension=0, tiled=True)
    square_sum = lax.psum_scatter(local_squares, ("fy", "fc"), scatter_dimension=0, tiled=True)
    inv_rms = lax.rsqrt(square_sum / (HEADS * HEAD_DIM) + 1e-06)
    return (summed.astype(jnp.float32) * inv_rms[:, None]).astype(jnp.bfloat16)


def split_mesh(mesh):
    devices = mesh.devices
    seq, fsdp = devices.shape
    chips_x = 8 if seq % 8 == 0 else 1
    cores = 2 if fsdp % 2 == 0 else 1
    grid = devices.reshape(seq // chips_x, chips_x, fsdp // cores, cores)
    return jax.sharding.Mesh(grid, ("sz", "sx", "fy", "fc"))


def solution(mesh):
    fine = split_mesh(mesh)
    seq = ("sz", "sx")
    fsdp = ("fy", "fc")
    placed = (
        P(seq, fsdp),
        P(seq, fsdp),
        P(seq, fsdp),
        P(seq, fsdp),
        P(fsdp),
        P(fsdp),
        P(fsdp, None),
    )
    return jax.shard_map(
        per_device, mesh=fine, in_specs=placed, out_specs=P(seq + fsdp, None), check_vma=False
    )
```

```python
import math

import jax
import jax.numpy as jnp
from jax import lax
from jax.sharding import PartitionSpec as P

HEADS = 64
HEAD_DIM = 128


layer_factor = 1.0 - 78.0 / 79.0 + 1e-05


def decay_slopes(rate_index):
    exponent = -8.0 * (rate_index.astype(jnp.float32) + 1.0) / HEADS
    return jnp.exp(exponent * math.log(2.0)) * layer_factor


def span_terms(query_rows, key_rows, value_rows, slopes):
    tok_count = query_rows.shape[0]
    position = jnp.arange(tok_count).astype(jnp.float32)
    offset = position[:, None] - position[None, :]
    causal = jnp.where(
        offset[None] >= 0.0, jnp.exp(-slopes[:, None, None] * jnp.maximum(offset, 0.0)[None]), 0.0
    )
    scores = jnp.einsum("thd,shd->hts", query_rows, key_rows, preferred_element_type=jnp.float32)
    weighted = (scores * causal).astype(jnp.bfloat16)
    intra_part = jnp.einsum(
        "hts,she->the", weighted, value_rows, preferred_element_type=jnp.float32
    )
    to_end = jnp.exp(-slopes[None, :] * (tok_count - 1.0 - position)[:, None])
    key_scaled = (key_rows.astype(jnp.float32) * to_end[:, :, None]).astype(jnp.bfloat16)
    local_state = jnp.einsum(
        "thd,the->hde", key_scaled, value_rows, preferred_element_type=jnp.float32
    )
    from_start = jnp.exp(-slopes[None, :] * (position + 1.0)[:, None])
    return (intra_part, local_state, from_start)


def decayed_scan(local_state, slopes, tok_count):
    chips_x = lax.axis_size("sx")
    chips_z = lax.axis_size("sz")
    x = lax.axis_index("sx")
    z = lax.axis_index("sz")
    rate = slopes[None, :] * tok_count
    row = lax.all_gather(local_state.astype(jnp.bfloat16), "sx").astype(jnp.float32)
    xs = jnp.arange(chips_x)
    before = jnp.where(
        (xs < x)[:, None], jnp.exp(-rate * jnp.maximum(x - 1 - xs, 0).astype(jnp.float32)[:, None]), 0.0
    )
    to_end = jnp.exp(-rate * (chips_x - 1 - xs).astype(jnp.float32)[:, None])
    in_row = jnp.sum(before[:, :, None, None] * row, axis=0)
    row_total = jnp.sum(to_end[:, :, None, None] * row, axis=0)
    column = lax.all_gather(row_total.astype(jnp.bfloat16), "sz").astype(jnp.float32)
    zs = jnp.arange(chips_z)
    steps = chips_x * jnp.maximum(z - 1 - zs, 0) + x
    earlier = jnp.where((zs < z)[:, None], jnp.exp(-rate * steps.astype(jnp.float32)[:, None]), 0.0)
    return in_row + jnp.sum(earlier[:, :, None, None] * column, axis=0)


def per_device(query_act, key_act, value_act, gate_act, rate_index, norm_gain, out_weight):
    tok_count = query_act.shape[0]
    heads_here = rate_index.shape[0]
    slopes = decay_slopes(rate_index)
    span_shape = (tok_count, heads_here, HEAD_DIM)
    query_rows = query_act.reshape(span_shape)
    key_rows = key_act.reshape(span_shape)
    value_rows = value_act.reshape(span_shape)
    gate_rows = gate_act.reshape(span_shape)
    gain_table = norm_gain.reshape(heads_here, HEAD_DIM)
    intra_part, local_state, from_start = span_terms(query_rows, key_rows, value_rows, slopes)
    incoming = decayed_scan(local_state, slopes, tok_count)
    inter_part = jnp.einsum(
        "thd,hde->the", query_rows.astype(jnp.float32), incoming, precision=lax.Precision.HIGHEST
    )
    attended = intra_part + from_start[:, :, None] * inter_part
    local_squares = jnp.sum(attended * attended, axis=(1, 2))
    gated = attended * gain_table[None] * jax.nn.sigmoid(gate_rows.astype(jnp.float32))
    gated = gated.reshape(tok_count, -1).astype(jnp.bfloat16)
    projected = jnp.dot(gated, out_weight, preferred_element_type=jnp.float32).astype(jnp.bfloat16)
    summed = lax.psum_scatter(projected, ("fy", "fc"), scatter_dimension=0, tiled=True)
    square_sum = lax.psum_scatter(local_squares, ("fy", "fc"), scatter_dimension=0, tiled=True)
    inv_rms = lax.rsqrt(square_sum / (HEADS * HEAD_DIM) + 1e-06)
    return (summed.astype(jnp.float32) * inv_rms[:, None]).astype(jnp.bfloat16)


def split_mesh(mesh):
    devices = mesh.devices
    seq, fsdp = devices.shape
    chips_x = 8 if seq % 8 == 0 else 1
    cores = 2 if fsdp % 2 == 0 else 1
    grid = devices.reshape(seq // chips_x, chips_x, fsdp // cores, cores)
    return jax.sharding.Mesh(grid, ("sz", "sx", "fy", "fc"))


def solution(mesh):
    fine = split_mesh(mesh)
    seq = ("sz", "sx")
    fsdp = ("fy", "fc")
    placed = (
        P(seq, fsdp),
        P(seq, fsdp),
        P(seq, fsdp),
        P(seq, fsdp),
        P(fsdp),
        P(fsdp),
        P(fsdp, None),
    )
    return jax.shard_map(
        per_device, mesh=fine, in_specs=placed, out_specs=P(seq + fsdp, None), check_vma=False
    )
```

```python
import math

import jax
import jax.numpy as jnp
from jax import lax
from jax.sharding import PartitionSpec as P

HEADS = 64
HEAD_DIM = 128


layer_factor = 1.0 - 78.0 / 79.0 + 1e-05


def decay_slopes(rate_index):
    exponent = -8.0 * (rate_index.astype(jnp.float32) + 1.0) / HEADS
    return jnp.exp(exponent * math.log(2.0)) * layer_factor


def span_terms(query_rows, key_rows, value_rows, slopes):
    tok_count = query_rows.shape[0]
    position = jnp.arange(tok_count).astype(jnp.float32)
    offset = position[:, None] - position[None, :]
    causal = jnp.where(
        offset[None] >= 0.0, jnp.exp(-slopes[:, None, None] * jnp.maximum(offset, 0.0)[None]), 0.0
    )
    scores = jnp.einsum("thd,shd->hts", query_rows, key_rows, preferred_element_type=jnp.float32)
    weighted = (scores * causal).astype(jnp.bfloat16)
    intra_part = jnp.einsum(
        "hts,she->the", weighted, value_rows, preferred_element_type=jnp.float32
    )
    to_end = jnp.exp(-slopes[None, :] * (tok_count - 1.0 - position)[:, None])
    key_scaled = (key_rows.astype(jnp.float32) * to_end[:, :, None]).astype(jnp.bfloat16)
    local_state = jnp.einsum(
        "thd,the->hde", key_scaled, value_rows, preferred_element_type=jnp.float32
    )
    from_start = jnp.exp(-slopes[None, :] * (position + 1.0)[:, None])
    return (intra_part, local_state, from_start)


def decayed_scan(local_state, slopes, tok_count, axis):
    peers = lax.axis_size(axis)
    total = local_state
    shift = 1
    while shift < peers:
        decay = jnp.exp(-slopes * (tok_count * shift))
        moved = lax.ppermute(total, axis, perm=[(i, i + shift) for i in range(peers - shift)])
        total = total + decay[:, None, None] * moved
        shift *= 2
    undo = jnp.exp(slopes * tok_count)
    return (total - local_state) * undo[:, None, None]


def fsdp_reduce(parts):
    chips = lax.axis_size("fy")
    core = lax.axis_index("fc")
    chip = lax.axis_index("fy")
    keep = lax.dynamic_index_in_dim(parts, core, axis=1, keepdims=False)
    give = lax.dynamic_index_in_dim(parts, 1 - core, axis=1, keepdims=False)
    got = lax.ppermute(give, "fc", perm=[(0, 1), (1, 0)])
    mine = keep.astype(jnp.float32) + got.astype(jnp.float32)
    half = mine.shape[2] // 2
    halves = []
    for sign, cols in ((1, slice(0, half)), (-1, slice(half, None))):
        blocks = mine[:, :, cols]
        pairs = [(j, (j + sign) % chips) for j in range(chips)]
        cur = lax.dynamic_index_in_dim(blocks, (chip - sign) % chips, axis=0, keepdims=False)
        for k in range(chips - 1):
            recv = lax.ppermute(cur.astype(jnp.bfloat16), "fy", perm=pairs)
            own = lax.dynamic_index_in_dim(blocks, (chip - sign * (k + 2)) % chips, axis=0, keepdims=False)
            cur = recv.astype(jnp.float32) + own
        halves.append(cur)
    return jnp.concatenate(halves, axis=1)


def per_device(query_act, key_act, value_act, gate_act, rate_index, norm_gain, out_weight):
    tok_count = query_act.shape[0]
    heads_here = rate_index.shape[0]
    slopes = decay_slopes(rate_index)
    span_shape = (tok_count, heads_here, HEAD_DIM)
    query_rows = query_act.reshape(span_shape)
    key_rows = key_act.reshape(span_shape)
    value_rows = value_act.reshape(span_shape)
    gate_rows = gate_act.reshape(span_shape)
    gain_table = norm_gain.reshape(heads_here, HEAD_DIM)
    intra_part, local_state, from_start = span_terms(query_rows, key_rows, value_rows, slopes)
    incoming = decayed_scan(local_state, slopes, tok_count, ("sz", "sx"))
    inter_part = jnp.einsum(
        "thd,hde->the", query_rows.astype(jnp.float32), incoming, precision=lax.Precision.HIGHEST
    )
    attended = intra_part + from_start[:, :, None] * inter_part
    local_squares = jnp.sum(attended * attended, axis=(1, 2))
    gated = attended * gain_table[None] * jax.nn.sigmoid(gate_rows.astype(jnp.float32))
    gated = gated.reshape(tok_count, -1).astype(jnp.bfloat16)
    projected = jnp.dot(gated, out_weight, preferred_element_type=jnp.float32).astype(jnp.bfloat16)
    summed = fsdp_reduce(projected.reshape(-1, 2, tok_count // 16, projected.shape[1]))
    gathered = lax.all_gather(local_squares, ("fy", "fc"))
    owner = lax.axis_index("fy") * lax.axis_size("fc") + lax.axis_index("fc")
    rows = summed.shape[0]
    square_sum = lax.dynamic_slice_in_dim(jnp.sum(gathered, axis=0), owner * rows, rows)
    inv_rms = lax.rsqrt(square_sum / (HEADS * HEAD_DIM) + 1e-06)
    return (summed.astype(jnp.float32) * inv_rms[:, None]).astype(jnp.bfloat16)


def split_mesh(mesh):
    devices = mesh.devices
    seq, fsdp = devices.shape
    chips_x = 8 if seq % 8 == 0 else 1
    cores = 2 if fsdp % 2 == 0 else 1
    grid = devices.reshape(seq // chips_x, chips_x, fsdp // cores, cores)
    return jax.sharding.Mesh(grid, ("sz", "sx", "fy", "fc"))


def solution(mesh):
    fine = split_mesh(mesh)
    seq = ("sz", "sx")
    fsdp = ("fy", "fc")
    placed = (
        P(seq, fsdp),
        P(seq, fsdp),
        P(seq, fsdp),
        P(seq, fsdp),
        P(fsdp),
        P(fsdp),
        P(fsdp, None),
    )
    return jax.shard_map(
        per_device, mesh=fine, in_specs=placed, out_specs=P(seq + fsdp, None), check_vma=False
    )
```

```python
import math

import jax
import jax.numpy as jnp
from jax import lax
from jax.sharding import PartitionSpec as P

HEADS = 64
HEAD_DIM = 128


layer_factor = 1.0 - 78.0 / 79.0 + 1e-05


def decay_slopes(rate_index):
    exponent = -8.0 * (rate_index.astype(jnp.float32) + 1.0) / HEADS
    return jnp.exp(exponent * math.log(2.0)) * layer_factor


def span_terms(query_rows, key_rows, value_rows, slopes):
    tok_count = query_rows.shape[0]
    position = jnp.arange(tok_count).astype(jnp.float32)
    offset = position[:, None] - position[None, :]
    causal = jnp.where(
        offset[None] >= 0.0, jnp.exp(-slopes[:, None, None] * jnp.maximum(offset, 0.0)[None]), 0.0
    )
    scores = jnp.einsum("thd,shd->hts", query_rows, key_rows, preferred_element_type=jnp.float32)
    weighted = (scores * causal).astype(jnp.bfloat16)
    intra_part = jnp.einsum(
        "hts,she->the", weighted, value_rows, preferred_element_type=jnp.float32
    )
    to_end = jnp.exp(-slopes[None, :] * (tok_count - 1.0 - position)[:, None])
    key_scaled = (key_rows.astype(jnp.float32) * to_end[:, :, None]).astype(jnp.bfloat16)
    local_state = jnp.einsum(
        "thd,the->hde", key_scaled, value_rows, preferred_element_type=jnp.float32
    )
    from_start = jnp.exp(-slopes[None, :] * (position + 1.0)[:, None])
    return (intra_part, local_state, from_start)


def decayed_scan(local_state, slopes, tok_count, axis):
    peers = lax.axis_size(axis)
    total = local_state
    shift = 1
    while shift < peers:
        decay = jnp.exp(-slopes * (tok_count * shift))
        moved = lax.ppermute(total, axis, perm=[(i, i + shift) for i in range(peers - shift)])
        total = total + decay[:, None, None] * moved
        shift *= 2
    undo = jnp.exp(slopes * tok_count)
    return (total - local_state) * undo[:, None, None]


def pack(values, squares):
    hi = squares.astype(jnp.bfloat16)
    lo = (squares - hi.astype(jnp.float32)).astype(jnp.bfloat16)
    pad = jnp.zeros(squares.shape + (126,), jnp.bfloat16)
    extra = jnp.concatenate([hi[..., None], lo[..., None], pad], axis=-1)
    return jnp.concatenate([values.astype(jnp.bfloat16), extra], axis=-1)


def unpack(packed, lanes):
    squares = packed[..., lanes].astype(jnp.float32) + packed[..., lanes + 1].astype(jnp.float32)
    return packed[..., :lanes].astype(jnp.float32), squares


def fsdp_reduce(parts, squares):
    chips = lax.axis_size("fy")
    core = lax.axis_index("fc")
    chip = lax.axis_index("fy")
    lanes = parts.shape[-1]
    keep = lax.dynamic_index_in_dim(parts, core, axis=1, keepdims=False)
    keep_sq = lax.dynamic_index_in_dim(squares, core, axis=1, keepdims=False)
    give = lax.dynamic_index_in_dim(parts, 1 - core, axis=1, keepdims=False)
    give_sq = lax.dynamic_index_in_dim(squares, 1 - core, axis=1, keepdims=False)
    got, got_sq = unpack(lax.ppermute(pack(give, give_sq), "fc", perm=[(0, 1), (1, 0)]), lanes)
    mine = keep.astype(jnp.float32) + got
    mine_sq = keep_sq + got_sq
    pairs = [(j, (j + 1) % chips) for j in range(chips)]
    cur = lax.dynamic_index_in_dim(mine, (chip - 1) % chips, axis=0, keepdims=False)
    cur_sq = lax.dynamic_index_in_dim(mine_sq, (chip - 1) % chips, axis=0, keepdims=False)
    for k in range(chips - 1):
        recv, recv_sq = unpack(lax.ppermute(pack(cur, cur_sq), "fy", perm=pairs), lanes)
        index = (chip - k - 2) % chips
        cur = recv + lax.dynamic_index_in_dim(mine, index, axis=0, keepdims=False)
        cur_sq = recv_sq + lax.dynamic_index_in_dim(mine_sq, index, axis=0, keepdims=False)
    return cur, cur_sq


def per_device(query_act, key_act, value_act, gate_act, rate_index, norm_gain, out_weight):
    tok_count = query_act.shape[0]
    heads_here = rate_index.shape[0]
    slopes = decay_slopes(rate_index)
    span_shape = (tok_count, heads_here, HEAD_DIM)
    query_rows = query_act.reshape(span_shape)
    key_rows = key_act.reshape(span_shape)
    value_rows = value_act.reshape(span_shape)
    gate_rows = gate_act.reshape(span_shape)
    gain_table = norm_gain.reshape(heads_here, HEAD_DIM)
    intra_part, local_state, from_start = span_terms(query_rows, key_rows, value_rows, slopes)
    incoming = decayed_scan(local_state, slopes, tok_count, ("sz", "sx"))
    inter_part = jnp.einsum(
        "thd,hde->the", query_rows.astype(jnp.float32), incoming, precision=lax.Precision.HIGHEST
    )
    attended = intra_part + from_start[:, :, None] * inter_part
    local_squares = jnp.sum(attended * attended, axis=(1, 2))
    gated = attended * gain_table[None] * jax.nn.sigmoid(gate_rows.astype(jnp.float32))
    gated = gated.reshape(tok_count, -1).astype(jnp.bfloat16)
    projected = jnp.dot(gated, out_weight, preferred_element_type=jnp.float32).astype(jnp.bfloat16)
    owned = tok_count // 16
    summed, square_sum = fsdp_reduce(
        projected.reshape(-1, 2, owned, projected.shape[1]), local_squares.reshape(-1, 2, owned)
    )
    inv_rms = lax.rsqrt(square_sum / (HEADS * HEAD_DIM) + 1e-06)
    return (summed.astype(jnp.float32) * inv_rms[:, None]).astype(jnp.bfloat16)


def split_mesh(mesh):
    devices = mesh.devices
    seq, fsdp = devices.shape
    chips_x = 8 if seq % 8 == 0 else 1
    cores = 2 if fsdp % 2 == 0 else 1
    grid = devices.reshape(seq // chips_x, chips_x, fsdp // cores, cores)
    return jax.sharding.Mesh(grid, ("sz", "sx", "fy", "fc"))


def solution(mesh):
    fine = split_mesh(mesh)
    seq = ("sz", "sx")
    fsdp = ("fy", "fc")
    placed = (
        P(seq, fsdp),
        P(seq, fsdp),
        P(seq, fsdp),
        P(seq, fsdp),
        P(fsdp),
        P(fsdp),
        P(fsdp, None),
    )
    return jax.shard_map(
        per_device, mesh=fine, in_specs=placed, out_specs=P(seq + fsdp, None), check_vma=False
    )
```

```python
import math

import jax
import jax.numpy as jnp
from jax import lax
from jax.sharding import PartitionSpec as P

HEADS = 64
HEAD_DIM = 128


layer_factor = 1.0 - 78.0 / 79.0 + 1e-05


def decay_slopes(rate_index):
    exponent = -8.0 * (rate_index.astype(jnp.float32) + 1.0) / HEADS
    return jnp.exp(exponent * math.log(2.0)) * layer_factor


def span_terms(query_rows, key_rows, value_rows, slopes):
    tok_count = query_rows.shape[0]
    position = jnp.arange(tok_count).astype(jnp.float32)
    offset = position[:, None] - position[None, :]
    causal = jnp.where(
        offset[None] >= 0.0, jnp.exp(-slopes[:, None, None] * jnp.maximum(offset, 0.0)[None]), 0.0
    )
    scores = jnp.einsum("thd,shd->hts", query_rows, key_rows, preferred_element_type=jnp.float32)
    weighted = (scores * causal).astype(jnp.bfloat16)
    intra_part = jnp.einsum(
        "hts,she->the", weighted, value_rows, preferred_element_type=jnp.float32
    )
    to_end = jnp.exp(-slopes[None, :] * (tok_count - 1.0 - position)[:, None])
    key_scaled = (key_rows.astype(jnp.float32) * to_end[:, :, None]).astype(jnp.bfloat16)
    local_state = jnp.einsum(
        "thd,the->hde", key_scaled, value_rows, preferred_element_type=jnp.float32
    )
    from_start = jnp.exp(-slopes[None, :] * (position + 1.0)[:, None])
    return (intra_part, local_state, from_start)


def decayed_scan(local_state, slopes, tok_count, axis):
    peers = lax.axis_size(axis)
    total = local_state
    shift = 1
    while shift < peers:
        decay = jnp.exp(-slopes * (tok_count * shift))
        moved = lax.ppermute(total, axis, perm=[(i, i + shift) for i in range(peers - shift)])
        total = total + decay[:, None, None] * moved
        shift *= 2
    undo = jnp.exp(slopes * tok_count)
    return (total - local_state) * undo[:, None, None]


def pack(values, squares):
    hi = squares.astype(jnp.bfloat16)
    lo = (squares - hi.astype(jnp.float32)).astype(jnp.bfloat16)
    pad = jnp.zeros(squares.shape + (126,), jnp.bfloat16)
    extra = jnp.concatenate([hi[..., None], lo[..., None], pad], axis=-1)
    return jnp.concatenate([values.astype(jnp.bfloat16), extra], axis=-1)


def unpack(packed, lanes):
    squares = packed[..., lanes].astype(jnp.float32) + packed[..., lanes + 1].astype(jnp.float32)
    return packed[..., :lanes].astype(jnp.float32), squares


def fsdp_reduce(parts, squares):
    core = lax.axis_index("fc")
    lanes = parts.shape[-1]
    keep = lax.dynamic_index_in_dim(parts, core, axis=1, keepdims=False)
    keep_sq = lax.dynamic_index_in_dim(squares, core, axis=1, keepdims=False)
    give = lax.dynamic_index_in_dim(parts, 1 - core, axis=1, keepdims=False)
    give_sq = lax.dynamic_index_in_dim(squares, 1 - core, axis=1, keepdims=False)
    got, got_sq = unpack(lax.ppermute(pack(give, give_sq), "fc", perm=[(0, 1), (1, 0)]), lanes)
    mine = keep.astype(jnp.float32) + got
    mine_sq = keep_sq + got_sq
    moved = lax.all_to_all(pack(mine, mine_sq), "fy", 0, 0, tiled=True)
    values, sums = unpack(moved, lanes)
    cur = jnp.sum(values, axis=0)
    cur_sq = jnp.sum(sums, axis=0)
    return cur, cur_sq


def per_device(query_act, key_act, value_act, gate_act, rate_index, norm_gain, out_weight):
    tok_count = query_act.shape[0]
    heads_here = rate_index.shape[0]
    slopes = decay_slopes(rate_index)
    span_shape = (tok_count, heads_here, HEAD_DIM)
    query_rows = query_act.reshape(span_shape)
    key_rows = key_act.reshape(span_shape)
    value_rows = value_act.reshape(span_shape)
    gate_rows = gate_act.reshape(span_shape)
    gain_table = norm_gain.reshape(heads_here, HEAD_DIM)
    intra_part, local_state, from_start = span_terms(query_rows, key_rows, value_rows, slopes)
    incoming = decayed_scan(local_state, slopes, tok_count, ("sz", "sx"))
    inter_part = jnp.einsum(
        "thd,hde->the", query_rows.astype(jnp.float32), incoming, precision=lax.Precision.HIGHEST
    )
    attended = intra_part + from_start[:, :, None] * inter_part
    local_squares = jnp.sum(attended * attended, axis=(1, 2))
    gated = attended * gain_table[None] * jax.nn.sigmoid(gate_rows.astype(jnp.float32))
    gated = gated.reshape(tok_count, -1).astype(jnp.bfloat16)
    projected = jnp.dot(gated, out_weight, preferred_element_type=jnp.float32).astype(jnp.bfloat16)
    owned = tok_count // 16
    summed, square_sum = fsdp_reduce(
        projected.reshape(-1, 2, owned, projected.shape[1]), local_squares.reshape(-1, 2, owned)
    )
    inv_rms = lax.rsqrt(square_sum / (HEADS * HEAD_DIM) + 1e-06)
    return (summed.astype(jnp.float32) * inv_rms[:, None]).astype(jnp.bfloat16)


def split_mesh(mesh):
    devices = mesh.devices
    seq, fsdp = devices.shape
    chips_x = 8 if seq % 8 == 0 else 1
    cores = 2 if fsdp % 2 == 0 else 1
    grid = devices.reshape(seq // chips_x, chips_x, fsdp // cores, cores)
    return jax.sharding.Mesh(grid, ("sz", "sx", "fy", "fc"))


def solution(mesh):
    fine = split_mesh(mesh)
    seq = ("sz", "sx")
    fsdp = ("fy", "fc")
    placed = (
        P(seq, fsdp),
        P(seq, fsdp),
        P(seq, fsdp),
        P(seq, fsdp),
        P(fsdp),
        P(fsdp),
        P(fsdp, None),
    )
    return jax.shard_map(
        per_device, mesh=fine, in_specs=placed, out_specs=P(seq + fsdp, None), check_vma=False
    )
```

```python
import math

import jax
import jax.numpy as jnp
from jax import lax
from jax.sharding import PartitionSpec as P

HEADS = 64
HEAD_DIM = 128


layer_factor = 1.0 - 78.0 / 79.0 + 1e-05


def decay_slopes(rate_index):
    exponent = -8.0 * (rate_index.astype(jnp.float32) + 1.0) / HEADS
    return jnp.exp(exponent * math.log(2.0)) * layer_factor


def span_terms(query_rows, key_rows, value_rows, slopes):
    tok_count = query_rows.shape[0]
    position = jnp.arange(tok_count).astype(jnp.float32)
    offset = position[:, None] - position[None, :]
    causal = jnp.where(
        offset[None] >= 0.0, jnp.exp(-slopes[:, None, None] * jnp.maximum(offset, 0.0)[None]), 0.0
    )
    scores = jnp.einsum("thd,shd->hts", query_rows, key_rows, preferred_element_type=jnp.float32)
    weighted = (scores * causal).astype(jnp.bfloat16)
    intra_part = jnp.einsum(
        "hts,she->the", weighted, value_rows, preferred_element_type=jnp.float32
    )
    to_end = jnp.exp(-slopes[None, :] * (tok_count - 1.0 - position)[:, None])
    key_scaled = (key_rows.astype(jnp.float32) * to_end[:, :, None]).astype(jnp.bfloat16)
    local_state = jnp.einsum(
        "thd,the->hde", key_scaled, value_rows, preferred_element_type=jnp.float32
    )
    from_start = jnp.exp(-slopes[None, :] * (position + 1.0)[:, None])
    return (intra_part, local_state, from_start)


def decayed_scan(local_state, slopes, tok_count, axis):
    peers = lax.axis_size(axis)
    total = local_state
    earlier = jnp.zeros_like(local_state)
    shift = 1
    while shift < peers:
        decay = jnp.exp(-slopes * (tok_count * shift))
        moved = lax.ppermute(
            total.astype(jnp.bfloat16), axis, perm=[(i, i + shift) for i in range(peers - shift)]
        )
        part = decay[:, None, None] * moved.astype(jnp.float32)
        earlier = earlier + part
        total = total + part
        shift *= 2
    undo = jnp.exp(slopes * tok_count)
    return earlier * undo[:, None, None]


def pack(values, squares):
    hi = squares.astype(jnp.bfloat16)
    lo = (squares - hi.astype(jnp.float32)).astype(jnp.bfloat16)
    pad = jnp.zeros(squares.shape + (126,), jnp.bfloat16)
    extra = jnp.concatenate([hi[..., None], lo[..., None], pad], axis=-1)
    return jnp.concatenate([values.astype(jnp.bfloat16), extra], axis=-1)


def unpack(packed, lanes):
    squares = packed[..., lanes].astype(jnp.float32) + packed[..., lanes + 1].astype(jnp.float32)
    return packed[..., :lanes].astype(jnp.float32), squares


def fsdp_reduce(parts, squares):
    core = lax.axis_index("fc")
    lanes = parts.shape[-1]
    keep = lax.dynamic_index_in_dim(parts, core, axis=1, keepdims=False)
    keep_sq = lax.dynamic_index_in_dim(squares, core, axis=1, keepdims=False)
    give = lax.dynamic_index_in_dim(parts, 1 - core, axis=1, keepdims=False)
    give_sq = lax.dynamic_index_in_dim(squares, 1 - core, axis=1, keepdims=False)
    got, got_sq = unpack(lax.ppermute(pack(give, give_sq), "fc", perm=[(0, 1), (1, 0)]), lanes)
    mine = keep.astype(jnp.float32) + got
    mine_sq = keep_sq + got_sq
    moved = lax.all_to_all(pack(mine, mine_sq), "fy", 0, 0, tiled=True)
    values, sums = unpack(moved, lanes)
    cur = jnp.sum(values, axis=0)
    cur_sq = jnp.sum(sums, axis=0)
    return cur, cur_sq


def per_device(query_act, key_act, value_act, gate_act, rate_index, norm_gain, out_weight):
    tok_count = query_act.shape[0]
    heads_here = rate_index.shape[0]
    slopes = decay_slopes(rate_index)
    span_shape = (tok_count, heads_here, HEAD_DIM)
    query_rows = query_act.reshape(span_shape)
    key_rows = key_act.reshape(span_shape)
    value_rows = value_act.reshape(span_shape)
    gate_rows = gate_act.reshape(span_shape)
    gain_table = norm_gain.reshape(heads_here, HEAD_DIM)
    intra_part, local_state, from_start = span_terms(query_rows, key_rows, value_rows, slopes)
    incoming = decayed_scan(local_state, slopes, tok_count, ("sz", "sx"))
    inter_part = jnp.einsum(
        "thd,hde->the", query_rows.astype(jnp.float32), incoming, precision=lax.Precision.HIGHEST
    )
    attended = intra_part + from_start[:, :, None] * inter_part
    local_squares = jnp.sum(attended * attended, axis=(1, 2))
    gated = attended * gain_table[None] * jax.nn.sigmoid(gate_rows.astype(jnp.float32))
    gated = gated.reshape(tok_count, -1).astype(jnp.bfloat16)
    projected = jnp.dot(gated, out_weight, preferred_element_type=jnp.float32).astype(jnp.bfloat16)
    owned = tok_count // 16
    summed, square_sum = fsdp_reduce(
        projected.reshape(-1, 2, owned, projected.shape[1]), local_squares.reshape(-1, 2, owned)
    )
    inv_rms = lax.rsqrt(square_sum / (HEADS * HEAD_DIM) + 1e-06)
    return (summed.astype(jnp.float32) * inv_rms[:, None]).astype(jnp.bfloat16)


def split_mesh(mesh):
    devices = mesh.devices
    seq, fsdp = devices.shape
    chips_x = 8 if seq % 8 == 0 else 1
    cores = 2 if fsdp % 2 == 0 else 1
    grid = devices.reshape(seq // chips_x, chips_x, fsdp // cores, cores)
    return jax.sharding.Mesh(grid, ("sz", "sx", "fy", "fc"))


def solution(mesh):
    fine = split_mesh(mesh)
    seq = ("sz", "sx")
    fsdp = ("fy", "fc")
    placed = (
        P(seq, fsdp),
        P(seq, fsdp),
        P(seq, fsdp),
        P(seq, fsdp),
        P(fsdp),
        P(fsdp),
        P(fsdp, None),
    )
    return jax.shard_map(
        per_device, mesh=fine, in_specs=placed, out_specs=P(seq + fsdp, None), check_vma=False
    )
```

```python
import math

import jax
import jax.numpy as jnp
from jax import lax
from jax.sharding import PartitionSpec as P

HEADS = 64
HEAD_DIM = 128


layer_factor = 1.0 - 78.0 / 79.0 + 1e-05


def decay_slopes(rate_index):
    exponent = -8.0 * (rate_index.astype(jnp.float32) + 1.0) / HEADS
    return jnp.exp(exponent * math.log(2.0)) * layer_factor


def span_terms(query_rows, key_rows, value_rows, slopes):
    tok_count = query_rows.shape[0]
    position = jnp.arange(tok_count).astype(jnp.float32)
    offset = position[:, None] - position[None, :]
    causal = jnp.where(
        offset[None] >= 0.0, jnp.exp(-slopes[:, None, None] * jnp.maximum(offset, 0.0)[None]), 0.0
    )
    scores = jnp.einsum("thd,shd->hts", query_rows, key_rows, preferred_element_type=jnp.float32)
    weighted = (scores * causal).astype(jnp.bfloat16)
    intra_part = jnp.einsum(
        "hts,she->the", weighted, value_rows, preferred_element_type=jnp.float32
    )
    to_end = jnp.exp(-slopes[None, :] * (tok_count - 1.0 - position)[:, None])
    key_scaled = (key_rows.astype(jnp.float32) * to_end[:, :, None]).astype(jnp.bfloat16)
    local_state = jnp.einsum(
        "thd,the->hde", key_scaled, value_rows, preferred_element_type=jnp.float32
    )
    from_start = jnp.exp(-slopes[None, :] * (position + 1.0)[:, None])
    return (intra_part, local_state, from_start)


def decayed_scan(local_state, slopes, tok_count, axis):
    peers = lax.axis_size(axis)
    total = local_state
    earlier = jnp.zeros_like(local_state)
    shift = 1
    while shift < peers:
        decay = jnp.exp(-slopes * (tok_count * shift))
        moved = lax.ppermute(
            total.astype(jnp.bfloat16), axis, perm=[(i, i + shift) for i in range(peers - shift)]
        )
        part = decay[:, None, None] * moved.astype(jnp.float32)
        earlier = earlier + part
        total = total + part
        shift *= 2
    undo = jnp.exp(slopes * tok_count)
    return earlier * undo[:, None, None]


def pack(values, squares):
    hi = squares.astype(jnp.bfloat16)
    lo = (squares - hi.astype(jnp.float32)).astype(jnp.bfloat16)
    pad = jnp.zeros(squares.shape + (126,), jnp.bfloat16)
    extra = jnp.concatenate([hi[..., None], lo[..., None], pad], axis=-1)
    return jnp.concatenate([values.astype(jnp.bfloat16), extra], axis=-1)


def unpack(packed, lanes):
    squares = packed[..., lanes].astype(jnp.float32) + packed[..., lanes + 1].astype(jnp.float32)
    return packed[..., :lanes].astype(jnp.float32), squares


def fsdp_reduce(gated, squares, weight):
    core = lax.axis_index("fc")
    chips, _, rows, features = gated.shape
    lanes = weight.shape[1]

    def project(block):
        flat = jnp.dot(block.reshape(-1, features), weight, preferred_element_type=jnp.float32)
        return flat.astype(jnp.bfloat16).reshape(chips, rows, lanes)

    give = project(lax.dynamic_index_in_dim(gated, 1 - core, axis=1, keepdims=False))
    give_sq = lax.dynamic_index_in_dim(squares, 1 - core, axis=1, keepdims=False)
    sent = lax.ppermute(pack(give, give_sq), "fc", perm=[(0, 1), (1, 0)])
    keep = project(lax.dynamic_index_in_dim(gated, core, axis=1, keepdims=False))
    keep_sq = lax.dynamic_index_in_dim(squares, core, axis=1, keepdims=False)
    got, got_sq = unpack(sent, lanes)
    mine = keep.astype(jnp.float32) + got
    mine_sq = keep_sq + got_sq
    moved = lax.all_to_all(pack(mine, mine_sq), "fy", 0, 0, tiled=True)
    values, sums = unpack(moved, lanes)
    return jnp.sum(values, axis=0), jnp.sum(sums, axis=0)


def per_device(query_act, key_act, value_act, gate_act, rate_index, norm_gain, out_weight):
    tok_count = query_act.shape[0]
    heads_here = rate_index.shape[0]
    slopes = decay_slopes(rate_index)
    span_shape = (tok_count, heads_here, HEAD_DIM)
    query_rows = query_act.reshape(span_shape)
    key_rows = key_act.reshape(span_shape)
    value_rows = value_act.reshape(span_shape)
    gate_rows = gate_act.reshape(span_shape)
    gain_table = norm_gain.reshape(heads_here, HEAD_DIM)
    intra_part, local_state, from_start = span_terms(query_rows, key_rows, value_rows, slopes)
    incoming = decayed_scan(local_state, slopes, tok_count, ("sz", "sx"))
    inter_part = jnp.einsum(
        "thd,hde->the", query_rows.astype(jnp.float32), incoming, precision=lax.Precision.HIGHEST
    )
    attended = intra_part + from_start[:, :, None] * inter_part
    local_squares = jnp.sum(attended * attended, axis=(1, 2))
    gated = attended * gain_table[None] * jax.nn.sigmoid(gate_rows.astype(jnp.float32))
    gated = gated.reshape(tok_count, -1).astype(jnp.bfloat16)
    owned = tok_count // 16
    summed, square_sum = fsdp_reduce(
        gated.reshape(-1, 2, owned, gated.shape[1]), local_squares.reshape(-1, 2, owned), out_weight
    )
    inv_rms = lax.rsqrt(square_sum / (HEADS * HEAD_DIM) + 1e-06)
    return (summed.astype(jnp.float32) * inv_rms[:, None]).astype(jnp.bfloat16)


def split_mesh(mesh):
    devices = mesh.devices
    seq, fsdp = devices.shape
    chips_x = 8 if seq % 8 == 0 else 1
    cores = 2 if fsdp % 2 == 0 else 1
    grid = devices.reshape(seq // chips_x, chips_x, fsdp // cores, cores)
    return jax.sharding.Mesh(grid, ("sz", "sx", "fy", "fc"))


def solution(mesh):
    fine = split_mesh(mesh)
    seq = ("sz", "sx")
    fsdp = ("fy", "fc")
    placed = (
        P(seq, fsdp),
        P(seq, fsdp),
        P(seq, fsdp),
        P(seq, fsdp),
        P(fsdp),
        P(fsdp),
        P(fsdp, None),
    )
    return jax.shard_map(
        per_device, mesh=fine, in_specs=placed, out_specs=P(seq + fsdp, None), check_vma=False
    )
```

```python
import math

import jax
import jax.numpy as jnp
from jax import lax
from jax.sharding import PartitionSpec as P

HEADS = 64
HEAD_DIM = 128


layer_factor = 1.0 - 78.0 / 79.0 + 1e-05


def decay_slopes(rate_index):
    exponent = -8.0 * (rate_index.astype(jnp.float32) + 1.0) / HEADS
    return jnp.exp(exponent * math.log(2.0)) * layer_factor


def span_terms(query_rows, key_rows, value_rows, slopes):
    tok_count = query_rows.shape[0]
    position = jnp.arange(tok_count).astype(jnp.float32)
    offset = position[:, None] - position[None, :]
    causal = jnp.where(
        offset[None] >= 0.0, jnp.exp(-slopes[:, None, None] * jnp.maximum(offset, 0.0)[None]), 0.0
    )
    scores = jnp.einsum("thd,shd->hts", query_rows, key_rows, preferred_element_type=jnp.float32)
    weighted = (scores * causal).astype(jnp.bfloat16)
    intra_part = jnp.einsum(
        "hts,she->the", weighted, value_rows, preferred_element_type=jnp.float32
    )
    to_end = jnp.exp(-slopes[None, :] * (tok_count - 1.0 - position)[:, None])
    key_scaled = (key_rows.astype(jnp.float32) * to_end[:, :, None]).astype(jnp.bfloat16)
    local_state = jnp.einsum(
        "thd,the->hde", key_scaled, value_rows, preferred_element_type=jnp.float32
    )
    from_start = jnp.exp(-slopes[None, :] * (position + 1.0)[:, None])
    return (intra_part, local_state, from_start)


def decayed_scan(local_state, slopes, tok_count, axis):
    peers = lax.axis_size(axis)
    total = local_state
    earlier = jnp.zeros_like(local_state)
    shift = 1
    while shift < peers:
        decay = jnp.exp(-slopes * (tok_count * shift))
        moved = lax.ppermute(
            total.astype(jnp.bfloat16), axis, perm=[(i, i + shift) for i in range(peers - shift)]
        )
        part = decay[:, None, None] * moved.astype(jnp.float32)
        earlier = earlier + part
        total = total + part
        shift *= 2
    undo = jnp.exp(slopes * tok_count)
    return earlier * undo[:, None, None]


def pack(values, squares):
    hi = squares.astype(jnp.bfloat16)
    lo = (squares - hi.astype(jnp.float32)).astype(jnp.bfloat16)
    pad = jnp.zeros(squares.shape + (126,), jnp.bfloat16)
    extra = jnp.concatenate([hi[..., None], lo[..., None], pad], axis=-1)
    return jnp.concatenate([values.astype(jnp.bfloat16), extra], axis=-1)


def unpack(packed, lanes):
    squares = packed[..., lanes].astype(jnp.float32) + packed[..., lanes + 1].astype(jnp.float32)
    return packed[..., :lanes].astype(jnp.float32), squares


def fsdp_reduce(gated, squares, weight):
    core = lax.axis_index("fc")
    chips, _, rows, features = gated.shape
    lanes = weight.shape[1]

    def project(block):
        flat = jnp.dot(block.reshape(-1, features), weight, preferred_element_type=jnp.float32)
        return flat.astype(jnp.bfloat16).reshape(chips, rows, lanes)

    give = project(lax.dynamic_index_in_dim(gated, 1 - core, axis=1, keepdims=False))
    give_sq = lax.dynamic_index_in_dim(squares, 1 - core, axis=1, keepdims=False)
    sent = lax.ppermute(pack(give, give_sq), "fc", perm=[(0, 1), (1, 0)])
    keep = project(lax.dynamic_index_in_dim(gated, core, axis=1, keepdims=False))
    keep_sq = lax.dynamic_index_in_dim(squares, core, axis=1, keepdims=False)
    got, got_sq = unpack(sent, lanes)
    mine = keep.astype(jnp.float32) + got
    mine_sq = keep_sq + got_sq
    return chip_ring(mine, mine_sq, lanes)


def chip_ring(mine, mine_sq, lanes):
    n = lax.axis_size("fy")
    i = lax.axis_index("fy")

    def block(j):
        return (
            lax.dynamic_index_in_dim(mine, j % n, axis=0, keepdims=False),
            lax.dynamic_index_in_dim(mine_sq, j % n, axis=0, keepdims=False),
        )

    ahead = [(j, (j + 1) % n) for j in range(n)]
    behind = [(j, (j - 1) % n) for j in range(n)]
    far = n // 2
    near = n - 1 - far
    cw, cw_sq = block(i + far)
    ccw, ccw_sq = block(i - near)
    for k in range(far):
        recv, recv_sq = unpack(lax.ppermute(pack(cw, cw_sq), "fy", perm=ahead), lanes)
        own, own_sq = block(i + far - 1 - k)
        cw, cw_sq = recv + own, recv_sq + own_sq
        if k < near:
            recv, recv_sq = unpack(lax.ppermute(pack(ccw, ccw_sq), "fy", perm=behind), lanes)
            if k < near - 1:
                own, own_sq = block(i - near + 1 + k)
                ccw, ccw_sq = recv + own, recv_sq + own_sq
            else:
                ccw, ccw_sq = recv, recv_sq
    return cw + ccw, cw_sq + ccw_sq


def per_device(query_act, key_act, value_act, gate_act, rate_index, norm_gain, out_weight):
    tok_count = query_act.shape[0]
    heads_here = rate_index.shape[0]
    slopes = decay_slopes(rate_index)
    span_shape = (tok_count, heads_here, HEAD_DIM)
    query_rows = query_act.reshape(span_shape)
    key_rows = key_act.reshape(span_shape)
    value_rows = value_act.reshape(span_shape)
    gate_rows = gate_act.reshape(span_shape)
    gain_table = norm_gain.reshape(heads_here, HEAD_DIM)
    intra_part, local_state, from_start = span_terms(query_rows, key_rows, value_rows, slopes)
    incoming = decayed_scan(local_state, slopes, tok_count, ("sz", "sx"))
    inter_part = jnp.einsum(
        "thd,hde->the", query_rows.astype(jnp.float32), incoming, precision=lax.Precision.HIGHEST
    )
    attended = intra_part + from_start[:, :, None] * inter_part
    local_squares = jnp.sum(attended * attended, axis=(1, 2))
    gated = attended * gain_table[None] * jax.nn.sigmoid(gate_rows.astype(jnp.float32))
    gated = gated.reshape(tok_count, -1).astype(jnp.bfloat16)
    owned = tok_count // 16
    summed, square_sum = fsdp_reduce(
        gated.reshape(-1, 2, owned, gated.shape[1]), local_squares.reshape(-1, 2, owned), out_weight
    )
    inv_rms = lax.rsqrt(square_sum / (HEADS * HEAD_DIM) + 1e-06)
    return (summed.astype(jnp.float32) * inv_rms[:, None]).astype(jnp.bfloat16)


def split_mesh(mesh):
    devices = mesh.devices
    seq, fsdp = devices.shape
    chips_x = 8 if seq % 8 == 0 else 1
    cores = 2 if fsdp % 2 == 0 else 1
    grid = devices.reshape(seq // chips_x, chips_x, fsdp // cores, cores)
    return jax.sharding.Mesh(grid, ("sz", "sx", "fy", "fc"))


def solution(mesh):
    fine = split_mesh(mesh)
    seq = ("sz", "sx")
    fsdp = ("fy", "fc")
    placed = (
        P(seq, fsdp),
        P(seq, fsdp),
        P(seq, fsdp),
        P(seq, fsdp),
        P(fsdp),
        P(fsdp),
        P(fsdp, None),
    )
    return jax.shard_map(
        per_device, mesh=fine, in_specs=placed, out_specs=P(seq + fsdp, None), check_vma=False
    )
```

```python
import math

import jax
import jax.numpy as jnp
from jax import lax
from jax.sharding import PartitionSpec as P

HEADS = 64
HEAD_DIM = 128


layer_factor = 1.0 - 78.0 / 79.0 + 1e-05


def decay_slopes(rate_index):
    exponent = -8.0 * (rate_index.astype(jnp.float32) + 1.0) / HEADS
    return jnp.exp(exponent * math.log(2.0)) * layer_factor


def span_terms(query_rows, key_rows, value_rows, slopes):
    tok_count = query_rows.shape[0]
    position = jnp.arange(tok_count).astype(jnp.float32)
    offset = position[:, None] - position[None, :]
    causal = jnp.where(
        offset[None] >= 0.0, jnp.exp(-slopes[:, None, None] * jnp.maximum(offset, 0.0)[None]), 0.0
    )
    scores = jnp.einsum("thd,shd->hts", query_rows, key_rows, preferred_element_type=jnp.float32)
    weighted = (scores * causal).astype(jnp.bfloat16)
    intra_part = jnp.einsum(
        "hts,she->the", weighted, value_rows, preferred_element_type=jnp.float32
    )
    to_end = jnp.exp(-slopes[None, :] * (tok_count - 1.0 - position)[:, None])
    key_scaled = (key_rows.astype(jnp.float32) * to_end[:, :, None]).astype(jnp.bfloat16)
    local_state = jnp.einsum(
        "thd,the->hde", key_scaled, value_rows, preferred_element_type=jnp.float32
    )
    from_start = jnp.exp(-slopes[None, :] * (position + 1.0)[:, None])
    return (intra_part, local_state, from_start)


def decayed_scan(local_state, slopes, tok_count, axis):
    peers = lax.axis_size(axis)
    total = local_state
    earlier = jnp.zeros_like(local_state)
    shift = 1
    while shift < peers:
        decay = jnp.exp(-slopes * (tok_count * shift))
        sent = total.astype(jnp.bfloat16)
        if shift * 2 == peers and lax.axis_size("sz") == 8:
            half = sent.shape[0] // 2
            ring = lax.axis_size("sz")
            hop = ring // 2
            direct = lax.ppermute(sent[:half], "sz", perm=[(z, z + hop) for z in range(hop)])
            back = lax.ppermute(sent[half:], "sz", perm=[(z, (z - 1) % ring) for z in range(hop)])
            back = lax.ppermute(back, "sz", perm=[((z - 1) % ring, z + hop) for z in range(hop)])
            moved = jnp.concatenate([direct, back], axis=0)
        else:
            moved = lax.ppermute(sent, axis, perm=[(i, i + shift) for i in range(peers - shift)])
        part = decay[:, None, None] * moved.astype(jnp.float32)
        earlier = earlier + part
        total = total + part
        shift *= 2
    undo = jnp.exp(slopes * tok_count)
    return earlier * undo[:, None, None]


def pack(values, squares):
    hi = squares.astype(jnp.bfloat16)
    lo = (squares - hi.astype(jnp.float32)).astype(jnp.bfloat16)
    pad = jnp.zeros(squares.shape + (126,), jnp.bfloat16)
    extra = jnp.concatenate([hi[..., None], lo[..., None], pad], axis=-1)
    return jnp.concatenate([values.astype(jnp.bfloat16), extra], axis=-1)


def unpack(packed, lanes):
    squares = packed[..., lanes].astype(jnp.float32) + packed[..., lanes + 1].astype(jnp.float32)
    return packed[..., :lanes].astype(jnp.float32), squares


def fsdp_reduce(gated, squares, weight):
    core = lax.axis_index("fc")
    chips, _, rows, features = gated.shape
    lanes = weight.shape[1]

    def project(block):
        flat = jnp.dot(block.reshape(-1, features), weight, preferred_element_type=jnp.float32)
        return flat.astype(jnp.bfloat16).reshape(chips, rows, lanes)

    give = project(lax.dynamic_index_in_dim(gated, 1 - core, axis=1, keepdims=False))
    give_sq = lax.dynamic_index_in_dim(squares, 1 - core, axis=1, keepdims=False)
    sent = lax.ppermute(pack(give, give_sq), "fc", perm=[(0, 1), (1, 0)])
    keep = project(lax.dynamic_index_in_dim(gated, core, axis=1, keepdims=False))
    keep_sq = lax.dynamic_index_in_dim(squares, core, axis=1, keepdims=False)
    got, got_sq = unpack(sent, lanes)
    mine = keep.astype(jnp.float32) + got
    mine_sq = keep_sq + got_sq
    moved = lax.all_to_all(pack(mine, mine_sq), "fy", 0, 0, tiled=True)
    values, sums = unpack(moved, lanes)
    return jnp.sum(values, axis=0), jnp.sum(sums, axis=0)


def per_device(query_act, key_act, value_act, gate_act, rate_index, norm_gain, out_weight):
    tok_count = query_act.shape[0]
    heads_here = rate_index.shape[0]
    slopes = decay_slopes(rate_index)
    span_shape = (tok_count, heads_here, HEAD_DIM)
    query_rows = query_act.reshape(span_shape)
    key_rows = key_act.reshape(span_shape)
    value_rows = value_act.reshape(span_shape)
    gate_rows = gate_act.reshape(span_shape)
    gain_table = norm_gain.reshape(heads_here, HEAD_DIM)
    intra_part, local_state, from_start = span_terms(query_rows, key_rows, value_rows, slopes)
    incoming = decayed_scan(local_state, slopes, tok_count, ("sz", "sx"))
    inter_part = jnp.einsum(
        "thd,hde->the", query_rows.astype(jnp.float32), incoming, precision=lax.Precision.HIGHEST
    )
    attended = intra_part + from_start[:, :, None] * inter_part
    local_squares = jnp.sum(attended * attended, axis=(1, 2))
    gated = attended * gain_table[None] * jax.nn.sigmoid(gate_rows.astype(jnp.float32))
    gated = gated.reshape(tok_count, -1).astype(jnp.bfloat16)
    owned = tok_count // 16
    summed, square_sum = fsdp_reduce(
        gated.reshape(-1, 2, owned, gated.shape[1]), local_squares.reshape(-1, 2, owned), out_weight
    )
    inv_rms = lax.rsqrt(square_sum / (HEADS * HEAD_DIM) + 1e-06)
    return (summed.astype(jnp.float32) * inv_rms[:, None]).astype(jnp.bfloat16)


def split_mesh(mesh):
    devices = mesh.devices
    seq, fsdp = devices.shape
    chips_x = 8 if seq % 8 == 0 else 1
    cores = 2 if fsdp % 2 == 0 else 1
    grid = devices.reshape(seq // chips_x, chips_x, fsdp // cores, cores)
    return jax.sharding.Mesh(grid, ("sz", "sx", "fy", "fc"))


def solution(mesh):
    fine = split_mesh(mesh)
    seq = ("sz", "sx")
    fsdp = ("fy", "fc")
    placed = (
        P(seq, fsdp),
        P(seq, fsdp),
        P(seq, fsdp),
        P(seq, fsdp),
        P(fsdp),
        P(fsdp),
        P(fsdp, None),
    )
    return jax.shard_map(
        per_device, mesh=fine, in_specs=placed, out_specs=P(seq + fsdp, None), check_vma=False
    )
```

```python
import math

import jax
import jax.numpy as jnp
from jax import lax
from jax.sharding import PartitionSpec as P

HEADS = 64
HEAD_DIM = 128


layer_factor = 1.0 - 78.0 / 79.0 + 1e-05


def decay_slopes(rate_index):
    exponent = -8.0 * (rate_index.astype(jnp.float32) + 1.0) / HEADS
    return jnp.exp(exponent * math.log(2.0)) * layer_factor


def span_terms(query_rows, key_rows, value_rows, slopes):
    tok_count = query_rows.shape[0]
    position = jnp.arange(tok_count).astype(jnp.float32)
    offset = position[:, None] - position[None, :]
    causal = jnp.where(
        offset[None] >= 0.0, jnp.exp(-slopes[:, None, None] * jnp.maximum(offset, 0.0)[None]), 0.0
    )
    scores = jnp.einsum("thd,shd->hts", query_rows, key_rows, preferred_element_type=jnp.float32)
    weighted = (scores * causal).astype(jnp.bfloat16)
    intra_part = jnp.einsum(
        "hts,she->the", weighted, value_rows, preferred_element_type=jnp.float32
    )
    to_end = jnp.exp(-slopes[None, :] * (tok_count - 1.0 - position)[:, None])
    key_scaled = (key_rows.astype(jnp.float32) * to_end[:, :, None]).astype(jnp.bfloat16)
    local_state = jnp.einsum(
        "thd,the->hde", key_scaled, value_rows, preferred_element_type=jnp.float32
    )
    from_start = jnp.exp(-slopes[None, :] * (position + 1.0)[:, None])
    return (intra_part, local_state, from_start)


def decayed_scan(local_state, slopes, tok_count, axis):
    peers = lax.axis_size(axis)
    total = local_state
    earlier = jnp.zeros_like(local_state)
    shift = 1
    while shift < peers:
        decay = jnp.exp(-slopes * (tok_count * shift))
        moved = lax.ppermute(
            total.astype(jnp.bfloat16), axis, perm=[(i, i + shift) for i in range(peers - shift)]
        )
        part = decay[:, None, None] * moved.astype(jnp.float32)
        earlier = earlier + part
        total = total + part
        shift *= 2
    undo = jnp.exp(slopes * tok_count)
    return earlier * undo[:, None, None]


def pack(values, squares):
    hi = squares.astype(jnp.bfloat16)
    lo = (squares - hi.astype(jnp.float32)).astype(jnp.bfloat16)
    pad = jnp.zeros(squares.shape + (126,), jnp.bfloat16)
    extra = jnp.concatenate([hi[..., None], lo[..., None], pad], axis=-1)
    return jnp.concatenate([values.astype(jnp.bfloat16), extra], axis=-1)


def unpack(packed, lanes):
    squares = packed[..., lanes].astype(jnp.float32) + packed[..., lanes + 1].astype(jnp.float32)
    return packed[..., :lanes].astype(jnp.float32), squares


def fsdp_reduce(gated, squares, weight):
    core = lax.axis_index("fc")
    chips, _, rows, features = gated.shape
    lanes = weight.shape[1]

    def project(block):
        flat = jnp.dot(block.reshape(-1, features), weight, preferred_element_type=jnp.float32)
        return flat.astype(jnp.bfloat16).reshape(chips, rows, lanes)

    give = project(lax.dynamic_index_in_dim(gated, 1 - core, axis=1, keepdims=False))
    give_sq = lax.dynamic_index_in_dim(squares, 1 - core, axis=1, keepdims=False)
    sent = lax.ppermute(pack(give, give_sq), "fc", perm=[(0, 1), (1, 0)])
    keep = project(lax.dynamic_index_in_dim(gated, core, axis=1, keepdims=False))
    keep_sq = lax.dynamic_index_in_dim(squares, core, axis=1, keepdims=False)
    got, got_sq = unpack(sent, lanes)
    mine = keep.astype(jnp.float32) + got
    mine_sq = keep_sq + got_sq
    values = lax.all_to_all(mine.astype(jnp.bfloat16), "fy", 0, 0, tiled=True)
    sums = lax.all_to_all(mine_sq, "fy", 0, 0, tiled=True)
    return jnp.sum(values.astype(jnp.float32), axis=0), jnp.sum(sums, axis=0)


def per_device(query_act, key_act, value_act, gate_act, rate_index, norm_gain, out_weight):
    tok_count = query_act.shape[0]
    heads_here = rate_index.shape[0]
    slopes = decay_slopes(rate_index)
    span_shape = (tok_count, heads_here, HEAD_DIM)
    query_rows = query_act.reshape(span_shape)
    key_rows = key_act.reshape(span_shape)
    value_rows = value_act.reshape(span_shape)
    gate_rows = gate_act.reshape(span_shape)
    gain_table = norm_gain.reshape(heads_here, HEAD_DIM)
    intra_part, local_state, from_start = span_terms(query_rows, key_rows, value_rows, slopes)
    incoming = decayed_scan(local_state, slopes, tok_count, ("sz", "sx"))
    inter_part = jnp.einsum(
        "thd,hde->the", query_rows.astype(jnp.float32), incoming, precision=lax.Precision.HIGHEST
    )
    attended = intra_part + from_start[:, :, None] * inter_part
    local_squares = jnp.sum(attended * attended, axis=(1, 2))
    gated = attended * gain_table[None] * jax.nn.sigmoid(gate_rows.astype(jnp.float32))
    gated = gated.reshape(tok_count, -1).astype(jnp.bfloat16)
    owned = tok_count // 16
    summed, square_sum = fsdp_reduce(
        gated.reshape(-1, 2, owned, gated.shape[1]), local_squares.reshape(-1, 2, owned), out_weight
    )
    inv_rms = lax.rsqrt(square_sum / (HEADS * HEAD_DIM) + 1e-06)
    return (summed.astype(jnp.float32) * inv_rms[:, None]).astype(jnp.bfloat16)


def split_mesh(mesh):
    devices = mesh.devices
    seq, fsdp = devices.shape
    chips_x = 8 if seq % 8 == 0 else 1
    cores = 2 if fsdp % 2 == 0 else 1
    grid = devices.reshape(seq // chips_x, chips_x, fsdp // cores, cores)
    return jax.sharding.Mesh(grid, ("sz", "sx", "fy", "fc"))


def solution(mesh):
    fine = split_mesh(mesh)
    seq = ("sz", "sx")
    fsdp = ("fy", "fc")
    placed = (
        P(seq, fsdp),
        P(seq, fsdp),
        P(seq, fsdp),
        P(seq, fsdp),
        P(fsdp),
        P(fsdp),
        P(fsdp, None),
    )
    return jax.shard_map(
        per_device, mesh=fine, in_specs=placed, out_specs=P(seq + fsdp, None), check_vma=False
    )
```

```python
import math

import jax
import jax.numpy as jnp
from jax import lax
from jax.sharding import PartitionSpec as P

HEADS = 64
HEAD_DIM = 128


layer_factor = 1.0 - 78.0 / 79.0 + 1e-05


def decay_slopes(rate_index):
    exponent = -8.0 * (rate_index.astype(jnp.float32) + 1.0) / HEADS
    return jnp.exp(exponent * math.log(2.0)) * layer_factor


def span_terms(query_rows, key_rows, value_rows, slopes):
    tok_count = query_rows.shape[0]
    position = jnp.arange(tok_count).astype(jnp.float32)
    offset = position[:, None] - position[None, :]
    causal = jnp.where(
        offset[None] >= 0.0, jnp.exp(-slopes[:, None, None] * jnp.maximum(offset, 0.0)[None]), 0.0
    )
    scores = jnp.einsum("thd,shd->hts", query_rows, key_rows, preferred_element_type=jnp.float32)
    weighted = (scores * causal).astype(jnp.bfloat16)
    intra_part = jnp.einsum(
        "hts,she->the", weighted, value_rows, preferred_element_type=jnp.float32
    )
    to_end = jnp.exp(-slopes[None, :] * (tok_count - 1.0 - position)[:, None])
    key_scaled = (key_rows.astype(jnp.float32) * to_end[:, :, None]).astype(jnp.bfloat16)
    local_state = jnp.einsum(
        "thd,the->hde", key_scaled, value_rows, preferred_element_type=jnp.float32
    )
    from_start = jnp.exp(-slopes[None, :] * (position + 1.0)[:, None])
    return (intra_part, local_state, from_start)


def decayed_scan(local_state, slopes, tok_count, axis):
    peers = lax.axis_size(axis)
    total = local_state
    earlier = jnp.zeros_like(local_state)
    shift = 1
    while shift < peers:
        decay = jnp.exp(-slopes * (tok_count * shift))
        moved = lax.ppermute(
            total.astype(jnp.bfloat16), axis, perm=[(i, i + shift) for i in range(peers - shift)]
        )
        part = decay[:, None, None] * moved.astype(jnp.float32)
        earlier = earlier + part
        total = total + part
        shift *= 2
    undo = jnp.exp(slopes * tok_count)
    return earlier * undo[:, None, None]


def pack(values, squares):
    hi = squares.astype(jnp.bfloat16)
    lo = (squares - hi.astype(jnp.float32)).astype(jnp.bfloat16)
    pad = jnp.zeros(squares.shape + (126,), jnp.bfloat16)
    extra = jnp.concatenate([hi[..., None], lo[..., None], pad], axis=-1)
    return jnp.concatenate([values.astype(jnp.bfloat16), extra], axis=-1)


def unpack(packed, lanes):
    squares = packed[..., lanes].astype(jnp.float32) + packed[..., lanes + 1].astype(jnp.float32)
    return packed[..., :lanes].astype(jnp.float32), squares


def fsdp_reduce(gated, squares, weight):
    core = lax.axis_index("fc")
    chips, _, rows, features = gated.shape
    lanes = weight.shape[1]

    def project(block):
        flat = jnp.dot(block.reshape(-1, features), weight, preferred_element_type=jnp.float32)
        return flat.astype(jnp.bfloat16).reshape(chips, rows, lanes)

    give = project(lax.dynamic_index_in_dim(gated, 1 - core, axis=1, keepdims=False))
    give_sq = lax.dynamic_index_in_dim(squares, 1 - core, axis=1, keepdims=False)
    sent = lax.ppermute(pack(give, give_sq), "fc", perm=[(0, 1), (1, 0)])
    keep = project(lax.dynamic_index_in_dim(gated, core, axis=1, keepdims=False))
    keep_sq = lax.dynamic_index_in_dim(squares, core, axis=1, keepdims=False)
    got, got_sq = unpack(sent, lanes)
    mine = keep.astype(jnp.float32) + got
    mine_sq = keep_sq + got_sq
    half = lanes // 2
    first = lax.all_to_all(pack(mine[:, :, :half], mine_sq), "fy", 0, 0, tiled=True)
    second = lax.all_to_all(mine[:, :, half:].astype(jnp.bfloat16), "fy", 0, 0, tiled=True)
    values, sums = unpack(first, half)
    out = jnp.concatenate([jnp.sum(values, axis=0), jnp.sum(second.astype(jnp.float32), axis=0)], axis=-1)
    return out, jnp.sum(sums, axis=0)


def per_device(query_act, key_act, value_act, gate_act, rate_index, norm_gain, out_weight):
    tok_count = query_act.shape[0]
    heads_here = rate_index.shape[0]
    slopes = decay_slopes(rate_index)
    span_shape = (tok_count, heads_here, HEAD_DIM)
    query_rows = query_act.reshape(span_shape)
    key_rows = key_act.reshape(span_shape)
    value_rows = value_act.reshape(span_shape)
    gate_rows = gate_act.reshape(span_shape)
    gain_table = norm_gain.reshape(heads_here, HEAD_DIM)
    intra_part, local_state, from_start = span_terms(query_rows, key_rows, value_rows, slopes)
    incoming = decayed_scan(local_state, slopes, tok_count, ("sz", "sx"))
    inter_part = jnp.einsum(
        "thd,hde->the", query_rows.astype(jnp.float32), incoming, precision=lax.Precision.HIGHEST
    )
    attended = intra_part + from_start[:, :, None] * inter_part
    local_squares = jnp.sum(attended * attended, axis=(1, 2))
    gated = attended * gain_table[None] * jax.nn.sigmoid(gate_rows.astype(jnp.float32))
    gated = gated.reshape(tok_count, -1).astype(jnp.bfloat16)
    owned = tok_count // 16
    summed, square_sum = fsdp_reduce(
        gated.reshape(-1, 2, owned, gated.shape[1]), local_squares.reshape(-1, 2, owned), out_weight
    )
    inv_rms = lax.rsqrt(square_sum / (HEADS * HEAD_DIM) + 1e-06)
    return (summed.astype(jnp.float32) * inv_rms[:, None]).astype(jnp.bfloat16)


def split_mesh(mesh):
    devices = mesh.devices
    seq, fsdp = devices.shape
    chips_x = 8 if seq % 8 == 0 else 1
    cores = 2 if fsdp % 2 == 0 else 1
    grid = devices.reshape(seq // chips_x, chips_x, fsdp // cores, cores)
    return jax.sharding.Mesh(grid, ("sz", "sx", "fy", "fc"))


def solution(mesh):
    fine = split_mesh(mesh)
    seq = ("sz", "sx")
    fsdp = ("fy", "fc")
    placed = (
        P(seq, fsdp),
        P(seq, fsdp),
        P(seq, fsdp),
        P(seq, fsdp),
        P(fsdp),
        P(fsdp),
        P(fsdp, None),
    )
    return jax.shard_map(
        per_device, mesh=fine, in_specs=placed, out_specs=P(seq + fsdp, None), check_vma=False
    )
```

```python
import math

import jax
import jax.numpy as jnp
from jax import lax
from jax.sharding import PartitionSpec as P

HEADS = 64
HEAD_DIM = 128


layer_factor = 1.0 - 78.0 / 79.0 + 1e-05


def decay_slopes(rate_index):
    exponent = -8.0 * (rate_index.astype(jnp.float32) + 1.0) / HEADS
    return jnp.exp(exponent * math.log(2.0)) * layer_factor


def span_terms(query_rows, key_rows, value_rows, slopes):
    tok_count = query_rows.shape[0]
    position = jnp.arange(tok_count).astype(jnp.float32)
    offset = position[:, None] - position[None, :]
    causal = jnp.where(
        offset[None] >= 0.0, jnp.exp(-slopes[:, None, None] * jnp.maximum(offset, 0.0)[None]), 0.0
    )
    scores = jnp.einsum("thd,shd->hts", query_rows, key_rows, preferred_element_type=jnp.float32)
    weighted = (scores * causal).astype(jnp.bfloat16)
    intra_part = jnp.einsum(
        "hts,she->the", weighted, value_rows, preferred_element_type=jnp.float32
    )
    to_end = jnp.exp(-slopes[None, :] * (tok_count - 1.0 - position)[:, None])
    key_scaled = (key_rows.astype(jnp.float32) * to_end[:, :, None]).astype(jnp.bfloat16)
    local_state = jnp.einsum(
        "thd,the->hde", key_scaled, value_rows, preferred_element_type=jnp.float32
    )
    from_start = jnp.exp(-slopes[None, :] * (position + 1.0)[:, None])
    return (intra_part, local_state, from_start)


def decayed_scan(local_state, slopes, tok_count, axis):
    peers = lax.axis_size(axis)
    total = local_state
    earlier = jnp.zeros_like(local_state)
    shift = 1
    while shift < peers:
        decay = jnp.exp(-slopes * (tok_count * shift))
        moved = lax.ppermute(
            total.astype(jnp.bfloat16), axis, perm=[(i, i + shift) for i in range(peers - shift)]
        )
        part = decay[:, None, None] * moved.astype(jnp.float32)
        earlier = earlier + part
        total = total + part
        shift *= 2
    undo = jnp.exp(slopes * tok_count)
    return earlier * undo[:, None, None]


def pack(values, squares):
    hi = squares.astype(jnp.bfloat16)
    lo = (squares - hi.astype(jnp.float32)).astype(jnp.bfloat16)
    pad = jnp.zeros(squares.shape + (126,), jnp.bfloat16)
    extra = jnp.concatenate([hi[..., None], lo[..., None], pad], axis=-1)
    return jnp.concatenate([values.astype(jnp.bfloat16), extra], axis=-1)


def unpack(packed, lanes):
    squares = packed[..., lanes].astype(jnp.float32) + packed[..., lanes + 1].astype(jnp.float32)
    return packed[..., :lanes].astype(jnp.float32), squares


def fsdp_reduce(gated, squares, weight):
    core = lax.axis_index("fc")
    chips, _, rows, features = gated.shape
    lanes = weight.shape[1]

    def project(block):
        flat = jnp.dot(block.reshape(-1, features), weight, preferred_element_type=jnp.float32)
        return flat.astype(jnp.bfloat16).reshape(chips, rows, lanes)

    give = project(lax.dynamic_index_in_dim(gated, 1 - core, axis=1, keepdims=False))
    give_sq = lax.dynamic_index_in_dim(squares, 1 - core, axis=1, keepdims=False)
    sent = lax.ppermute(pack(give, give_sq), "fc", perm=[(0, 1), (1, 0)])
    keep = project(lax.dynamic_index_in_dim(gated, core, axis=1, keepdims=False))
    keep_sq = lax.dynamic_index_in_dim(squares, core, axis=1, keepdims=False)
    got, got_sq = unpack(sent, lanes)
    mine = keep.astype(jnp.float32) + got
    mine_sq = keep_sq + got_sq
    moved = lax.all_to_all(pack(mine, mine_sq), "fy", 0, 0, tiled=True)
    values, sums = unpack(moved, lanes)
    chip = lax.axis_index("fy")
    others = (jnp.arange(values.shape[0]) != chip)[:, None]
    own = lax.dynamic_index_in_dim(mine, chip, axis=0, keepdims=False)
    own_sq = lax.dynamic_index_in_dim(mine_sq, chip, axis=0, keepdims=False)
    total = jnp.sum(jnp.where(others[:, :, None], values, 0.0), axis=0) + own
    return total, jnp.sum(jnp.where(others, sums, 0.0), axis=0) + own_sq


def per_device(query_act, key_act, value_act, gate_act, rate_index, norm_gain, out_weight):
    tok_count = query_act.shape[0]
    heads_here = rate_index.shape[0]
    slopes = decay_slopes(rate_index)
    span_shape = (tok_count, heads_here, HEAD_DIM)
    query_rows = query_act.reshape(span_shape)
    key_rows = key_act.reshape(span_shape)
    value_rows = value_act.reshape(span_shape)
    gate_rows = gate_act.reshape(span_shape)
    gain_table = norm_gain.reshape(heads_here, HEAD_DIM)
    intra_part, local_state, from_start = span_terms(query_rows, key_rows, value_rows, slopes)
    incoming = decayed_scan(local_state, slopes, tok_count, ("sz", "sx"))
    inter_part = jnp.einsum(
        "thd,hde->the", query_rows.astype(jnp.float32), incoming, precision=lax.Precision.HIGHEST
    )
    attended = intra_part + from_start[:, :, None] * inter_part
    local_squares = jnp.sum(attended * attended, axis=(1, 2))
    gated = attended * gain_table[None] * jax.nn.sigmoid(gate_rows.astype(jnp.float32))
    gated = gated.reshape(tok_count, -1).astype(jnp.bfloat16)
    owned = tok_count // 16
    summed, square_sum = fsdp_reduce(
        gated.reshape(-1, 2, owned, gated.shape[1]), local_squares.reshape(-1, 2, owned), out_weight
    )
    inv_rms = lax.rsqrt(square_sum / (HEADS * HEAD_DIM) + 1e-06)
    return (summed.astype(jnp.float32) * inv_rms[:, None]).astype(jnp.bfloat16)


def split_mesh(mesh):
    devices = mesh.devices
    seq, fsdp = devices.shape
    chips_x = 8 if seq % 8 == 0 else 1
    cores = 2 if fsdp % 2 == 0 else 1
    grid = devices.reshape(seq // chips_x, chips_x, fsdp // cores, cores)
    return jax.sharding.Mesh(grid, ("sz", "sx", "fy", "fc"))


def solution(mesh):
    fine = split_mesh(mesh)
    seq = ("sz", "sx")
    fsdp = ("fy", "fc")
    placed = (
        P(seq, fsdp),
        P(seq, fsdp),
        P(seq, fsdp),
        P(seq, fsdp),
        P(fsdp),
        P(fsdp),
        P(fsdp, None),
    )
    return jax.shard_map(
        per_device, mesh=fine, in_specs=placed, out_specs=P(seq + fsdp, None), check_vma=False
    )
```

```python
import math

import jax
import jax.numpy as jnp
from jax import lax
from jax.sharding import PartitionSpec as P

HEADS = 64
HEAD_DIM = 128


layer_factor = 1.0 - 78.0 / 79.0 + 1e-05


def decay_slopes(rate_index):
    exponent = -8.0 * (rate_index.astype(jnp.float32) + 1.0) / HEADS
    return jnp.exp(exponent * math.log(2.0)) * layer_factor


def span_terms(query_rows, key_rows, value_rows, slopes):
    tok_count = query_rows.shape[0]
    position = jnp.arange(tok_count).astype(jnp.float32)
    offset = position[:, None] - position[None, :]
    causal = jnp.where(
        offset[None] >= 0.0, jnp.exp(-slopes[:, None, None] * jnp.maximum(offset, 0.0)[None]), 0.0
    )
    scores = jnp.einsum("thd,shd->hts", query_rows, key_rows, preferred_element_type=jnp.float32)
    weighted = (scores * causal).astype(jnp.bfloat16)
    intra_part = jnp.einsum(
        "hts,she->the", weighted, value_rows, preferred_element_type=jnp.float32
    )
    to_end = jnp.exp(-slopes[None, :] * (tok_count - 1.0 - position)[:, None])
    key_scaled = (key_rows.astype(jnp.float32) * to_end[:, :, None]).astype(jnp.bfloat16)
    heads = key_scaled.shape[1]
    full = lax.dot_general(
        key_scaled.reshape(tok_count, -1), value_rows.reshape(tok_count, -1),
        (((0,), (0,)), ((), ())), preferred_element_type=jnp.float32,
    ).reshape(heads, HEAD_DIM, heads, HEAD_DIM)
    local_state = jnp.stack([full[h, :, h] for h in range(heads)])
    from_start = jnp.exp(-slopes[None, :] * (position + 1.0)[:, None])
    return (intra_part, local_state, from_start)


def decayed_scan(local_state, slopes, tok_count, axis):
    peers = lax.axis_size(axis)
    total = local_state
    earlier = jnp.zeros_like(local_state)
    shift = 1
    while shift < peers:
        decay = jnp.exp(-slopes * (tok_count * shift))
        moved = lax.ppermute(
            total.astype(jnp.bfloat16), axis, perm=[(i, i + shift) for i in range(peers - shift)]
        )
        part = decay[:, None, None] * moved.astype(jnp.float32)
        earlier = earlier + part
        total = total + part
        shift *= 2
    undo = jnp.exp(slopes * tok_count)
    return earlier * undo[:, None, None]


def pack(values, squares):
    hi = squares.astype(jnp.bfloat16)
    lo = (squares - hi.astype(jnp.float32)).astype(jnp.bfloat16)
    pad = jnp.zeros(squares.shape + (126,), jnp.bfloat16)
    extra = jnp.concatenate([hi[..., None], lo[..., None], pad], axis=-1)
    return jnp.concatenate([values.astype(jnp.bfloat16), extra], axis=-1)


def unpack(packed, lanes):
    squares = packed[..., lanes].astype(jnp.float32) + packed[..., lanes + 1].astype(jnp.float32)
    return packed[..., :lanes].astype(jnp.float32), squares


def fsdp_reduce(gated, squares, weight):
    core = lax.axis_index("fc")
    chips, _, rows, features = gated.shape
    lanes = weight.shape[1]

    def project(block):
        flat = jnp.dot(block.reshape(-1, features), weight, preferred_element_type=jnp.float32)
        return flat.astype(jnp.bfloat16).reshape(chips, rows, lanes)

    give = project(lax.dynamic_index_in_dim(gated, 1 - core, axis=1, keepdims=False))
    give_sq = lax.dynamic_index_in_dim(squares, 1 - core, axis=1, keepdims=False)
    sent = lax.ppermute(pack(give, give_sq), "fc", perm=[(0, 1), (1, 0)])
    keep = project(lax.dynamic_index_in_dim(gated, core, axis=1, keepdims=False))
    keep_sq = lax.dynamic_index_in_dim(squares, core, axis=1, keepdims=False)
    got, got_sq = unpack(sent, lanes)
    mine = keep.astype(jnp.float32) + got
    mine_sq = keep_sq + got_sq
    moved = lax.all_to_all(pack(mine, mine_sq), "fy", 0, 0, tiled=True)
    values, sums = unpack(moved, lanes)
    return jnp.sum(values, axis=0), jnp.sum(sums, axis=0)


def per_device(query_act, key_act, value_act, gate_act, rate_index, norm_gain, out_weight):
    tok_count = query_act.shape[0]
    heads_here = rate_index.shape[0]
    slopes = decay_slopes(rate_index)
    span_shape = (tok_count, heads_here, HEAD_DIM)
    query_rows = query_act.reshape(span_shape)
    key_rows = key_act.reshape(span_shape)
    value_rows = value_act.reshape(span_shape)
    gate_rows = gate_act.reshape(span_shape)
    gain_table = norm_gain.reshape(heads_here, HEAD_DIM)
    intra_part, local_state, from_start = span_terms(query_rows, key_rows, value_rows, slopes)
    incoming = decayed_scan(local_state, slopes, tok_count, ("sz", "sx"))
    inter_part = jnp.einsum(
        "thd,hde->the", query_rows.astype(jnp.float32), incoming, precision=lax.Precision.HIGHEST
    )
    attended = intra_part + from_start[:, :, None] * inter_part
    local_squares = jnp.sum(attended * attended, axis=(1, 2))
    gated = attended * gain_table[None] * jax.nn.sigmoid(gate_rows.astype(jnp.float32))
    gated = gated.reshape(tok_count, -1).astype(jnp.bfloat16)
    owned = tok_count // 16
    summed, square_sum = fsdp_reduce(
        gated.reshape(-1, 2, owned, gated.shape[1]), local_squares.reshape(-1, 2, owned), out_weight
    )
    inv_rms = lax.rsqrt(square_sum / (HEADS * HEAD_DIM) + 1e-06)
    return (summed.astype(jnp.float32) * inv_rms[:, None]).astype(jnp.bfloat16)


def split_mesh(mesh):
    devices = mesh.devices
    seq, fsdp = devices.shape
    chips_x = 8 if seq % 8 == 0 else 1
    cores = 2 if fsdp % 2 == 0 else 1
    grid = devices.reshape(seq // chips_x, chips_x, fsdp // cores, cores)
    return jax.sharding.Mesh(grid, ("sz", "sx", "fy", "fc"))


def solution(mesh):
    fine = split_mesh(mesh)
    seq = ("sz", "sx")
    fsdp = ("fy", "fc")
    placed = (
        P(seq, fsdp),
        P(seq, fsdp),
        P(seq, fsdp),
        P(seq, fsdp),
        P(fsdp),
        P(fsdp),
        P(fsdp, None),
    )
    return jax.shard_map(
        per_device, mesh=fine, in_specs=placed, out_specs=P(seq + fsdp, None), check_vma=False
    )
```

```python
import math

import jax
import jax.numpy as jnp
from jax import lax
from jax.sharding import PartitionSpec as P

HEADS = 64
HEAD_DIM = 128


layer_factor = 1.0 - 78.0 / 79.0 + 1e-05


def decay_slopes(rate_index):
    exponent = -8.0 * (rate_index.astype(jnp.float32) + 1.0) / HEADS
    return jnp.exp(exponent * math.log(2.0)) * layer_factor


def span_terms(query_rows, key_rows, value_rows, slopes):
    tok_count = query_rows.shape[0]
    position = jnp.arange(tok_count).astype(jnp.float32)
    offset = position[:, None] - position[None, :]
    causal = jnp.where(
        offset[None] >= 0.0, jnp.exp(-slopes[:, None, None] * jnp.maximum(offset, 0.0)[None]), 0.0
    )
    scores = jnp.einsum("thd,shd->hts", query_rows, key_rows, preferred_element_type=jnp.float32)
    weighted = (scores * causal).astype(jnp.bfloat16)
    intra_part = jnp.einsum(
        "hts,she->the", weighted, value_rows, preferred_element_type=jnp.float32
    )
    to_end = jnp.exp(-slopes[None, :] * (tok_count - 1.0 - position)[:, None])
    key_scaled = (key_rows.astype(jnp.float32) * to_end[:, :, None]).astype(jnp.bfloat16)
    heads = key_scaled.shape[1]
    full = lax.dot_general(
        key_scaled.reshape(tok_count, -1), value_rows.reshape(tok_count, -1),
        (((0,), (0,)), ((), ())), preferred_element_type=jnp.float32,
    ).reshape(heads, HEAD_DIM, heads, HEAD_DIM)
    local_state = jnp.stack([full[h, :, h] for h in range(heads)])
    from_start = jnp.exp(-slopes[None, :] * (position + 1.0)[:, None])
    return (intra_part, local_state, from_start)


def decayed_scan(local_state, slopes, tok_count, axis):
    peers = lax.axis_size(axis)
    total = local_state
    earlier = jnp.zeros_like(local_state)
    shift = 1
    while shift < peers:
        decay = jnp.exp(-slopes * (tok_count * shift))
        moved = lax.ppermute(
            total.astype(jnp.bfloat16), axis, perm=[(i, i + shift) for i in range(peers - shift)]
        )
        part = decay[:, None, None] * moved.astype(jnp.float32)
        earlier = earlier + part
        total = total + part
        shift *= 2
    undo = jnp.exp(slopes * tok_count)
    return earlier * undo[:, None, None]


def pack(values, squares):
    hi = squares.astype(jnp.bfloat16)
    lo = (squares - hi.astype(jnp.float32)).astype(jnp.bfloat16)
    pad = jnp.zeros(squares.shape + (126,), jnp.bfloat16)
    extra = jnp.concatenate([hi[..., None], lo[..., None], pad], axis=-1)
    return jnp.concatenate([values.astype(jnp.bfloat16), extra], axis=-1)


def unpack(packed, lanes):
    squares = packed[..., lanes].astype(jnp.float32) + packed[..., lanes + 1].astype(jnp.float32)
    return packed[..., :lanes].astype(jnp.float32), squares


def fsdp_reduce(gated, squares, weight):
    core = lax.axis_index("fc")
    chips, _, rows, features = gated.shape
    lanes = weight.shape[1]

    def project(block):
        flat = jnp.dot(block.reshape(-1, features), weight, preferred_element_type=jnp.float32)
        return flat.astype(jnp.bfloat16).reshape(chips, rows, lanes)

    give = project(lax.dynamic_index_in_dim(gated, 1 - core, axis=1, keepdims=False))
    give_sq = lax.dynamic_index_in_dim(squares, 1 - core, axis=1, keepdims=False)
    sent = lax.ppermute(pack(give, give_sq), "fc", perm=[(0, 1), (1, 0)])
    keep = project(lax.dynamic_index_in_dim(gated, core, axis=1, keepdims=False))
    keep_sq = lax.dynamic_index_in_dim(squares, core, axis=1, keepdims=False)
    got, got_sq = unpack(sent, lanes)
    mine = keep.astype(jnp.float32) + got
    mine_sq = keep_sq + got_sq
    moved = lax.all_to_all(pack(mine, mine_sq), "fy", 0, 0, tiled=True)
    values, sums = unpack(moved, lanes)
    return jnp.sum(values, axis=0), jnp.sum(sums, axis=0)


def per_device(query_act, key_act, value_act, gate_act, rate_index, norm_gain, out_weight):
    tok_count = query_act.shape[0]
    heads_here = rate_index.shape[0]
    slopes = decay_slopes(rate_index)
    span_shape = (tok_count, heads_here, HEAD_DIM)
    query_rows = query_act.reshape(span_shape)
    key_rows = key_act.reshape(span_shape)
    value_rows = value_act.reshape(span_shape)
    gate_rows = gate_act.reshape(span_shape)
    gain_table = norm_gain.reshape(heads_here, HEAD_DIM)
    intra_part, local_state, from_start = span_terms(query_rows, key_rows, value_rows, slopes)
    incoming = decayed_scan(local_state, slopes, tok_count, ("sz", "sx"))
    state_hi = incoming.astype(jnp.bfloat16)
    state_lo = (incoming - state_hi.astype(jnp.float32)).astype(jnp.bfloat16)
    inter_part = jnp.einsum(
        "thd,hde->the", query_rows, state_hi, preferred_element_type=jnp.float32
    ) + jnp.einsum("thd,hde->the", query_rows, state_lo, preferred_element_type=jnp.float32)
    attended = intra_part + from_start[:, :, None] * inter_part
    local_squares = jnp.sum(attended * attended, axis=(1, 2))
    gated = attended * gain_table[None] * jax.nn.sigmoid(gate_rows.astype(jnp.float32))
    gated = gated.reshape(tok_count, -1).astype(jnp.bfloat16)
    owned = tok_count // 16
    summed, square_sum = fsdp_reduce(
        gated.reshape(-1, 2, owned, gated.shape[1]), local_squares.reshape(-1, 2, owned), out_weight
    )
    inv_rms = lax.rsqrt(square_sum / (HEADS * HEAD_DIM) + 1e-06)
    return (summed.astype(jnp.float32) * inv_rms[:, None]).astype(jnp.bfloat16)


def split_mesh(mesh):
    devices = mesh.devices
    seq, fsdp = devices.shape
    chips_x = 8 if seq % 8 == 0 else 1
    cores = 2 if fsdp % 2 == 0 else 1
    grid = devices.reshape(seq // chips_x, chips_x, fsdp // cores, cores)
    return jax.sharding.Mesh(grid, ("sz", "sx", "fy", "fc"))


def solution(mesh):
    fine = split_mesh(mesh)
    seq = ("sz", "sx")
    fsdp = ("fy", "fc")
    placed = (
        P(seq, fsdp),
        P(seq, fsdp),
        P(seq, fsdp),
        P(seq, fsdp),
        P(fsdp),
        P(fsdp),
        P(fsdp, None),
    )
    return jax.shard_map(
        per_device, mesh=fine, in_specs=placed, out_specs=P(seq + fsdp, None), check_vma=False
    )
```
